256 devices in a mesh: req: 128 (over y_hi, z, x, core), tp: 2 (over y_lo).
Axes of the slice: x: 4, y: 4 (y_hi: 2, y_lo: 2; y = y_hi * 2 + y_lo), z: 8, core: 2. Of those that a mesh axis runs over, the one named last changes fastest.
Arguments:
- tokens: bfloat16 [256, 512, 2048], P('req'), may hold values from -6 to 6
- qkv_master: float32 [2048, 3, 2048], P('req', None, 'tp')
- q_gain: float32 [2048], P('tp')
- k_gain: float32 [2048], P('tp')
- lengths: int32 [256], P('req'), may hold values from 1 to 512, as said below
- page_holder: int32 [256, 4], P('req'), may hold values from 0 to 127, as said below
- page_slot: int32 [256, 4], P('req'), may hold values from 0 to 2, as said below
Outputs:
- attended: bfloat16 [256, 512, 2048], P('req', None, 'tp')
- kv_cache: bfloat16 [1152, 2, 128, 2048], P('req', None, None, 'tp')
The draws below stay inside these ranges and needn't reach their ends.
Inputs may be any that keep to these rules, and one draw needn't show every extreme that they name: lengths[r] is at least 1; some prompt has exactly 512 tokens. page_holder[r, p] is r // 2, or the index just before or just after it along req, cyclically. The live pages of one req index's prompts that go to one holder have distinct page_slot values, so at most 3 of them; some req index sends 3 live pages to one holder.
All inputs are finite; a program needn't handle non-finite values.
Results may differ from the reference program's by a relative error of at most 0.009.
Values may be sent and summed in bfloat16 or wider, within the bound.
No kernel may reach another device: no remote copies, remote signals or barrier semaphores. Data moves between devices by JAX's collectives and lax.ppermute only.
A program may use at most 128 MiB of HBM per device.

```python
import math
import jax
import jax.numpy as jnp
from jax import lax

D = 2048
HEADS = 16
HD = 128
LEN = 512
PAGE = 128
REQ_DEV = 2
QDIM = 2048
PAGES = 4
CAP = 3
SLOTS = 9
REQS = 256
N_REQ = 128


def table_draw(key):
    first_factor = jax.random.randint(jax.random.fold_in(key, 101), (REQS,), 1, LEN + 1)
    second_factor = jax.random.randint(jax.random.fold_in(key, 102), (REQS,), 1, LEN + 1)
    chosen = jax.random.randint(jax.random.fold_in(key, 103), (), 0, REQS)
    request_ids = jnp.arange(REQS, dtype=jnp.int32)
    drawn_lengths = LEN + 1 - jnp.maximum(first_factor * second_factor // LEN, 1)
    drawn_lengths = jnp.where(request_ids == chosen, LEN, drawn_lengths).astype(jnp.int32)
    per_device = REQ_DEV * PAGES
    priority = jax.random.randint(jax.random.fold_in(key, 104), (N_REQ, SLOTS), 0, 1 << 20) * SLOTS + jnp.arange(SLOTS, dtype=jnp.int32)[None, :]
    slot_order = jnp.argsort(priority, axis=1)[:, :per_device].astype(jnp.int32)
    local_index = jnp.arange(per_device, dtype=jnp.int32)
    forced = SLOTS - 1 - (local_index - chosen % REQ_DEV * PAGES + per_device) % per_device
    device_ids = jnp.arange(N_REQ, dtype=jnp.int32)[:, None]
    slot_ids = jnp.where(device_ids == chosen // REQ_DEV, forced[None, :], slot_order)
    offsets = slot_ids // CAP - 1
    holders = (device_ids + offsets + N_REQ) % N_REQ
    within = slot_ids % CAP
    return (drawn_lengths, holders.reshape(REQS, PAGES).astype(jnp.int32), within.reshape(REQS, PAGES).astype(jnp.int32))


def draw_lengths(key, part):
    return table_draw(key)[0]


def draw_page_holder(key, part):
    return table_draw(key)[1]


def draw_page_slot(key, part):
    return table_draw(key)[2]


def draw_qkv_master(key, part):
    scale = D ** (-0.5)
    return jax.random.normal(jax.random.fold_in(key, 201), (D, 3, QDIM), jnp.float32) * scale


def gain_draw(key, salt):
    return jnp.exp(jax.random.uniform(jax.random.fold_in(key, salt), (QDIM,), jnp.float32, math.log(0.5), math.log(2.0)))


def draw_q_gain(key, part):
    return gain_draw(key, 302)


def draw_k_gain(key, part):
    return gain_draw(key, 303)


def block_scale(key, extent, pieces, smallest, largest):
    loudness, own = 1.0, jax.random.fold_in(key, 6)
    for position, shards_of in pieces:
        draws = jnp.exp(jax.random.uniform(jax.random.fold_in(own, position), (shards_of,), jnp.float32, smallest / len(pieces), largest / len(pieces)))
        loudness = loudness * jnp.repeat(draws, extent[position] // shards_of).reshape([-1 if axis == position else 1 for axis in range(len(extent))])
    return loudness


def centred(own_key, dims, width, most, cuts=(), kind=jnp.bfloat16):
    loudness = block_scale(own_key, dims, cuts, -0.22, 0.18) if cuts else 1.0
    drawn = jax.random.normal(own_key, dims, jnp.float32) * width * loudness
    return jnp.minimum(jnp.maximum(drawn, -most), most).astype(kind)


def setup_inputs(seed: int = 0) -> dict:
    splits = jax.random.split(jax.random.key(seed), 8)
    return {
        "tokens": centred(splits[0], (REQS, LEN, D), 1.0, 6.0, ((0, 128),)),
        "qkv_master": draw_qkv_master(jax.random.fold_in(splits[7], 71), 0),
        "q_gain": draw_q_gain(jax.random.fold_in(splits[7], 71), 0),
        "k_gain": draw_k_gain(jax.random.fold_in(splits[7], 71), 0),
        "lengths": draw_lengths(jax.random.fold_in(splits[7], 71), 0),
        "page_holder": draw_page_holder(jax.random.fold_in(splits[7], 71), 0),
        "page_slot": draw_page_slot(jax.random.fold_in(splits[7], 71), 0),
    }


norm_epsilon = 1e-06
rope_theta = 500000.0

def rotate(values_in, seq_len, head_size):
    half_size = head_size // 2
    positions = jnp.arange(seq_len).astype(jnp.float32)
    frequency = rope_theta ** (-jnp.arange(half_size).astype(jnp.float32) * 2.0 / head_size)
    angles = positions[:, None] * frequency[None, :]
    cosine_table = jnp.cos(angles)[:, None, :]
    sine_table = jnp.sin(angles)[:, None, :]
    front_half = values_in[..., :half_size]
    back_half = values_in[..., half_size:]
    return jnp.concatenate([front_half * cosine_table - back_half * sine_table, back_half * cosine_table + front_half * sine_table], -1)

def attend(queries, key_rows, value_rows, length):
    seq_len = queries.shape[0]
    scores = jnp.einsum('thd,uhd->htu', queries.astype(jnp.float32), key_rows.astype(jnp.float32)) * HD ** (-0.5)
    query_pos = jnp.arange(seq_len).astype(jnp.int32)[:, None]
    key_pos = jnp.arange(seq_len).astype(jnp.int32)[None, :]
    allowed = (key_pos <= query_pos) & (key_pos < length)
    scores = jnp.where(allowed[None], scores, -1e+30)
    row_max = lax.optimization_barrier(jnp.max(scores, axis=-1, keepdims=True))
    exp_terms = jnp.where(allowed[None], jnp.exp(scores - row_max), 0.0)
    probs = (exp_terms / lax.optimization_barrier(jnp.sum(exp_terms, axis=-1, keepdims=True))).astype(jnp.bfloat16)
    output = jnp.einsum('htu,uhd->thd', probs.astype(jnp.float32), value_rows.astype(jnp.float32))
    keep_rows = jnp.arange(seq_len).astype(jnp.int32)[:, None, None] < length
    return jnp.where(keep_rows, output, 0.0).astype(jnp.bfloat16)

def reference(tokens, qkv_master, q_gain, k_gain, lengths, page_holder, page_slot):
    weight = qkv_master.astype(jnp.bfloat16).reshape(D, 3 * QDIM)

    def single_request(request_item):
        token_rows, length = request_item
        projected = jnp.dot(token_rows, weight, preferred_element_type=jnp.float32)
        queries = projected[:, :QDIM]
        key_rows = projected[:, QDIM:2 * QDIM]
        values = projected[:, 2 * QDIM:]
        queries = queries * lax.rsqrt(lax.optimization_barrier(jnp.mean(queries * queries, -1, keepdims=True)) + norm_epsilon) * q_gain
        key_rows = key_rows * lax.rsqrt(lax.optimization_barrier(jnp.mean(key_rows * key_rows, -1, keepdims=True)) + norm_epsilon) * k_gain
        q_rot = rotate(queries.reshape(LEN, HEADS, HD), LEN, HD).astype(jnp.bfloat16)
        k_rot = rotate(key_rows.reshape(LEN, HEADS, HD), LEN, HD).astype(jnp.bfloat16)
        v_round = values.astype(jnp.bfloat16).reshape(LEN, HEADS, HD)
        output = attend(q_rot, k_rot, v_round, length)
        return (output.reshape(LEN, QDIM), k_rot.reshape(LEN, QDIM), v_round.reshape(LEN, QDIM))
    attended, keys_all, values_all = lax.map(single_request, (tokens, lengths))
    page_blocks = jnp.stack([keys_all.reshape(REQS, PAGES, PAGE, QDIM), values_all.reshape(REQS, PAGES, PAGE, QDIM)], axis=2)
    is_live = (jnp.arange(PAGES).astype(jnp.int32) * PAGE)[None, :] < lengths[:, None]
    home_index = (jnp.arange(REQS).astype(jnp.int32) // REQ_DEV)[:, None]
    offset = (page_holder - home_index + 1 + N_REQ) % N_REQ - 1
    target = jnp.where(is_live, page_holder * SLOTS + (offset + 1) * CAP + page_slot, N_REQ * SLOTS)
    cache_rows = jnp.zeros((N_REQ * SLOTS + 1, 2, PAGE, QDIM), jnp.bfloat16)
    cache_rows = cache_rows.at[target.reshape(-1)].set(page_blocks.reshape(REQS * PAGES, 2, PAGE, QDIM))
    return (attended, cache_rows[:N_REQ * SLOTS])
```

```python
import jax
import jax.numpy as jnp
from jax import lax
import numpy as np
from jax.sharding import Mesh, PartitionSpec as P

HD = 128
PAGE = 128
CAP = 3
SLOTS = 9


norm_epsilon = 1e-06
rope_theta = 500000.0


def _put(out, piece, idx, at, col=0):
    starts = [0] * out.ndim
    starts[at] = idx
    starts[-1] = col
    return lax.dynamic_update_slice(out, jnp.expand_dims(piece, at), starts)

def ring_gather(x, axis, n, me, at=0):
    out = jnp.zeros(x.shape[:at] + (n,) + x.shape[at:], x.dtype)
    out = _put(out, x, me, at)
    if n == 2:
        other = lax.ppermute(x, axis, [(0, 1), (1, 0)])
        return _put(out, other, 1 - me, at)
    fwd = [(i, (i + 1) % n) for i in range(n)]
    bwd = [((i + 1) % n, i) for i in range(n)]
    left, right = x, x
    half = n // 2
    for s in range(1, (n + 1) // 2):
        left = lax.ppermute(left, axis, fwd)
        right = lax.ppermute(right, axis, bwd)
        out = _put(out, left, (me - s) % n, at)
        out = _put(out, right, (me + s) % n, at)
    if n % 2 == 0:
        h = x.shape[-1] // 2
        a = lax.ppermute(left[..., :h], axis, fwd)
        b = lax.ppermute(right[..., h:], axis, bwd)
        j = (me + half) % n
        out = _put(out, a, j, at, 0)
        out = _put(out, b, j, at, h)
    return out

def weight_gather(b):
    yh, z, x, c = (lax.axis_index(a) for a in ("yh", "z", "x", "c"))
    g = ring_gather(b, "yh", 2, yh)
    ga = ring_gather(g[0], "x", 4, x)
    ga = ring_gather(ga, "z", 8, z)
    gb = ring_gather(g[1], "z", 8, z)
    gb = ring_gather(gb, "x", 4, x, at=1)
    own = jnp.stack([ga, gb])
    return ring_gather(own, "c", 2, c, at=3)


def extended(block, sides, width):
    for axis, dim in sides:
        count = lax.psum(1, axis)
        forward = [(i, i + 1) for i in range(count - 1)]
        forward.append((count - 1, 0))
        backward = [(target, source) for source, target in forward]
        low = lax.ppermute(
            lax.slice_in_dim(block, block.shape[dim] - width, None, axis=dim), axis, forward
        )
        high = lax.ppermute(lax.slice_in_dim(block, 0, width, axis=dim), axis, backward)
        block = jnp.concatenate([low, block, high], axis=dim)
    return block


def rotate(values_in, seq_len, head_size):
    half_size = head_size // 2
    positions = jnp.arange(seq_len).astype(jnp.float32)
    frequency = rope_theta ** (-jnp.arange(half_size).astype(jnp.float32) * 2.0 / head_size)
    angles = positions[:, None] * frequency[None, :]
    cosine_table = jnp.cos(angles)[:, None, :]
    sine_table = jnp.sin(angles)[:, None, :]
    front_half = values_in[..., :half_size]
    back_half = values_in[..., half_size:]
    return jnp.concatenate(
        [
            front_half * cosine_table - back_half * sine_table,
            back_half * cosine_table + front_half * sine_table,
        ],
        -1,
    )


def attend(request_item):
    queries, key_rows, value_rows, length = request_item
    seq_len = queries.shape[0]
    scores = jnp.einsum(
        "thd,uhd->htu", queries, key_rows, preferred_element_type=jnp.float32
    ) * HD ** (-0.5)
    query_pos = jnp.arange(seq_len)[:, None]
    key_pos = jnp.arange(seq_len)[None, :]
    allowed = (key_pos <= query_pos) & (key_pos < length)
    scores = jnp.where(allowed[None], scores, -1e30)
    row_max = jnp.max(scores, axis=-1, keepdims=True)
    exp_terms = jnp.where(allowed[None], jnp.exp(scores - row_max), 0.0)
    probs = (exp_terms / jnp.sum(exp_terms, axis=-1, keepdims=True)).astype(jnp.bfloat16)
    output = jnp.einsum("htu,uhd->thd", probs, value_rows, preferred_element_type=jnp.float32)
    keep_rows = jnp.arange(seq_len)[:, None, None] < length
    return jnp.where(keep_rows, output, 0.0).astype(jnp.bfloat16)


def body(tokens, qkv_master, q_gain, k_gain, lengths, page_holder, page_slot):
    req_dev, seq_len, model_width = tokens.shape
    row_share, _, q_local = qkv_master.shape
    heads_local = q_local // HD
    token_rows = tokens.reshape(req_dev * seq_len, model_width)
    master_local = qkv_master.astype(jnp.bfloat16).reshape(row_share, 3 * q_local)
    gathered = weight_gather(master_local).reshape(-1, master_local.shape[-1])
    projected = jnp.dot(token_rows, gathered, preferred_element_type=jnp.float32)
    queries = projected[:, :q_local]
    key_rows = projected[:, q_local : 2 * q_local]
    values = projected[:, 2 * q_local :]
    square_sums = lax.psum((jnp.sum(queries * queries, -1), jnp.sum(key_rows * key_rows, -1)), "tp")
    full_width = q_local * lax.axis_size("tp")
    queries = queries * lax.rsqrt(square_sums[0] / full_width + norm_epsilon)[:, None] * q_gain
    key_rows = key_rows * lax.rsqrt(square_sums[1] / full_width + norm_epsilon)[:, None] * k_gain
    q_rot = rotate(queries.reshape(req_dev, seq_len, heads_local, HD), seq_len, HD).astype(
        jnp.bfloat16
    )
    k_rot = rotate(key_rows.reshape(req_dev, seq_len, heads_local, HD), seq_len, HD).astype(
        jnp.bfloat16
    )
    v_round = values.astype(jnp.bfloat16).reshape(req_dev, seq_len, heads_local, HD)
    attended = lax.map(attend, (q_rot, k_rot, v_round, lengths)).reshape(req_dev, seq_len, q_local)
    page_count = seq_len // PAGE
    home_index = lax.axis_index(REQ)
    axis_count = lax.psum(1, REQ)
    is_live = (jnp.arange(page_count) * PAGE)[None, :] < lengths[:, None]
    offset = (page_holder - home_index + 1 + axis_count) % axis_count - 1
    target = jnp.where(is_live, (offset + 1) * CAP + page_slot, -1).reshape(-1)
    onehot = (target[None, :] == jnp.arange(SLOTS)[:, None]).astype(jnp.bfloat16)
    stacked = jnp.stack(
        [
            k_rot.reshape(req_dev * page_count, PAGE * q_local),
            v_round.reshape(req_dev * page_count, PAGE * q_local),
        ],
        1,
    )
    stacked = stacked.reshape(req_dev * page_count, 2 * PAGE * q_local)
    outgoing = (
        jnp.dot(onehot, stacked, preferred_element_type=jnp.float32)
        .astype(jnp.bfloat16)
        .reshape(SLOTS, 2, PAGE, q_local)
    )
    padded = extended(outgoing, ((REQ, 0),), CAP)
    kv_cache = jnp.concatenate([padded[CAP + SLOTS :], outgoing[CAP : 2 * CAP], padded[:CAP]], 0)
    return (attended, kv_cache)


REQ = ("yh", "z", "x", "c")


def solution(mesh):
    fine = Mesh(np.asarray(mesh.devices).reshape(2, 8, 4, 2, mesh.shape["tp"]), REQ + ("tp",))
    in_specs = (
        P(REQ, None, None),
        P(REQ, None, "tp"),
        P("tp"),
        P("tp"),
        P(REQ),
        P(REQ, None),
        P(REQ, None),
    )
    out_specs = (P(REQ, None, "tp"), P(REQ, None, None, "tp"))
    return jax.shard_map(body, mesh=fine, in_specs=in_specs, out_specs=out_specs, check_vma=False)
```

```python
import jax
import jax.numpy as jnp
from jax import lax
from jax.experimental import pallas as pl
from jax.experimental.pallas import tpu as pltpu
import numpy as np
from jax.sharding import Mesh, PartitionSpec as P

HD = 128
PAGE = 128
CAP = 3
SLOTS = 9


norm_epsilon = 1e-06
rope_theta = 500000.0


def _put(out, piece, idx, at, col=0):
    starts = [0] * out.ndim
    starts[at] = idx
    starts[-1] = col
    return lax.dynamic_update_slice(out, jnp.expand_dims(piece, at), starts)

def ring_gather(x, axis, n, me, at=0):
    out = jnp.zeros(x.shape[:at] + (n,) + x.shape[at:], x.dtype)
    out = _put(out, x, me, at)
    if n == 2:
        other = lax.ppermute(x, axis, [(0, 1), (1, 0)])
        return _put(out, other, 1 - me, at)
    fwd = [(i, (i + 1) % n) for i in range(n)]
    bwd = [((i + 1) % n, i) for i in range(n)]
    left, right = x, x
    half = n // 2
    for s in range(1, (n + 1) // 2):
        left = lax.ppermute(left, axis, fwd)
        right = lax.ppermute(right, axis, bwd)
        out = _put(out, left, (me - s) % n, at)
        out = _put(out, right, (me + s) % n, at)
    if n % 2 == 0:
        h = x.shape[-1] // 2
        a = lax.ppermute(left[..., :h], axis, fwd)
        b = lax.ppermute(right[..., h:], axis, bwd)
        j = (me + half) % n
        out = _put(out, a, j, at, 0)
        out = _put(out, b, j, at, h)
    return out

def weight_gather(b):
    yh, z, x, c = (lax.axis_index(a) for a in ("yh", "z", "x", "c"))
    g = ring_gather(b, "yh", 2, yh)
    ga = ring_gather(g[0], "x", 4, x)
    ga = ring_gather(ga, "z", 8, z)
    gb = ring_gather(g[1], "z", 8, z)
    gb = ring_gather(gb, "x", 4, x, at=1)
    own = jnp.stack([ga, gb])
    return ring_gather(own, "c", 2, c, at=3)


def attn_kernel(len_ref, q_ref, k_ref, v_ref, rq_ref, rk_ref, gq_ref, gk_ref, cos_ref, sin_ref,
                att_ref, krot_ref, vout_ref):
    length = len_ref[pl.program_id(0)]
    cos = cos_ref[...]
    sin = sin_ref[...]
    q = q_ref[...] * rq_ref[...] * gq_ref[...]
    k = k_ref[...] * rk_ref[...] * gk_ref[...]
    q_rot = (q * cos + pltpu.roll(q, HD // 2, 1) * sin).astype(jnp.bfloat16)
    k_rot = (k * cos + pltpu.roll(k, HD // 2, 1) * sin).astype(jnp.bfloat16)
    v = v_ref[...].astype(jnp.bfloat16)
    seq = q.shape[0]
    scores = lax.dot_general(q_rot, k_rot, (((1,), (1,)), ((), ())),
                             preferred_element_type=jnp.float32) * HD ** (-0.5)
    t = lax.broadcasted_iota(jnp.int32, (seq, seq), 0)
    u = lax.broadcasted_iota(jnp.int32, (seq, seq), 1)
    allowed = (u <= t) & (u < length)
    scores = jnp.where(allowed, scores, -1e30)
    row_max = jnp.max(scores, axis=-1, keepdims=True)
    exp_terms = jnp.where(allowed, jnp.exp(scores - row_max), 0.0)
    probs = (exp_terms / jnp.sum(exp_terms, axis=-1, keepdims=True)).astype(jnp.bfloat16)
    out = jnp.dot(probs, v, preferred_element_type=jnp.float32)
    rows = lax.broadcasted_iota(jnp.int32, (seq, 1), 0)
    att_ref[...] = jnp.where(rows < length, out, 0.0).astype(jnp.bfloat16)
    krot_ref[...] = k_rot
    vout_ref[...] = v


def fused_attention(projected, rq, rk, q_gain, k_gain, cos_full, sin_signed, lengths, req_dev, seq):
    q_local = projected.shape[1] // 3
    heads = q_local // HD
    blk = lambda off: pl.BlockSpec((seq, HD), lambda r, h, L: (r, off + h))
    row = pl.BlockSpec((seq, 1), lambda r, h, L: (r, 0))
    gain = pl.BlockSpec((1, HD), lambda r, h, L: (0, h))
    table = pl.BlockSpec((seq, HD), lambda r, h, L: (0, 0))
    out = pl.BlockSpec((seq, HD), lambda r, h, L: (r, h))
    shape = jax.ShapeDtypeStruct((req_dev * seq, q_local), jnp.bfloat16)
    steps = req_dev * heads
    cost = pl.CostEstimate(flops=steps * 4 * seq * seq * HD, transcendentals=steps * seq * seq,
                           bytes_accessed=steps * seq * HD * (3 * 4 + 3 * 2))
    return pl.pallas_call(
        attn_kernel,
        grid_spec=pltpu.PrefetchScalarGridSpec(
            num_scalar_prefetch=1,
            grid=(req_dev, heads),
            in_specs=[blk(0), blk(heads), blk(2 * heads), row, row, gain, gain, table, table],
            out_specs=[out, out, out],
        ),
        out_shape=[shape, shape, shape],
        cost_estimate=cost,
        name="fused_attention",
    )(lengths, projected, projected, projected, rq, rk, q_gain, k_gain, cos_full, sin_signed)


def extended(block, sides, width):
    for axis, dim in sides:
        count = lax.psum(1, axis)
        forward = [(i, i + 1) for i in range(count - 1)]
        forward.append((count - 1, 0))
        backward = [(target, source) for source, target in forward]
        low = lax.ppermute(
            lax.slice_in_dim(block, block.shape[dim] - width, None, axis=dim), axis, forward
        )
        high = lax.ppermute(lax.slice_in_dim(block, 0, width, axis=dim), axis, backward)
        block = jnp.concatenate([low, block, high], axis=dim)
    return block


def rotate(values_in, seq_len, head_size):
    half_size = head_size // 2
    positions = jnp.arange(seq_len).astype(jnp.float32)
    frequency = rope_theta ** (-jnp.arange(half_size).astype(jnp.float32) * 2.0 / head_size)
    angles = positions[:, None] * frequency[None, :]
    cosine_table = jnp.cos(angles)[:, None, :]
    sine_table = jnp.sin(angles)[:, None, :]
    front_half = values_in[..., :half_size]
    back_half = values_in[..., half_size:]
    return jnp.concatenate(
        [
            front_half * cosine_table - back_half * sine_table,
            back_half * cosine_table + front_half * sine_table,
        ],
        -1,
    )


def attend(request_item):
    queries, key_rows, value_rows, length = request_item
    seq_len = queries.shape[0]
    scores = jnp.einsum(
        "thd,uhd->htu", queries, key_rows, preferred_element_type=jnp.float32
    ) * HD ** (-0.5)
    query_pos = jnp.arange(seq_len)[:, None]
    key_pos = jnp.arange(seq_len)[None, :]
    allowed = (key_pos <= query_pos) & (key_pos < length)
    scores = jnp.where(allowed[None], scores, -1e30)
    row_max = jnp.max(scores, axis=-1, keepdims=True)
    exp_terms = jnp.where(allowed[None], jnp.exp(scores - row_max), 0.0)
    probs = (exp_terms / jnp.sum(exp_terms, axis=-1, keepdims=True)).astype(jnp.bfloat16)
    output = jnp.einsum("htu,uhd->thd", probs, value_rows, preferred_element_type=jnp.float32)
    keep_rows = jnp.arange(seq_len)[:, None, None] < length
    return jnp.where(keep_rows, output, 0.0).astype(jnp.bfloat16)


def body(tokens, qkv_master, q_gain, k_gain, lengths, page_holder, page_slot):
    req_dev, seq_len, model_width = tokens.shape
    row_share, _, q_local = qkv_master.shape
    heads_local = q_local // HD
    token_rows = tokens.reshape(req_dev * seq_len, model_width)
    master_local = qkv_master.astype(jnp.bfloat16).reshape(row_share, 3 * q_local)
    gathered = weight_gather(master_local).reshape(-1, master_local.shape[-1])
    projected = jnp.dot(token_rows, gathered, preferred_element_type=jnp.float32)
    square_sums = lax.psum(
        (
            jnp.sum(projected[:, :q_local] * projected[:, :q_local], -1),
            jnp.sum(projected[:, q_local : 2 * q_local] * projected[:, q_local : 2 * q_local], -1),
        ),
        "tp",
    )
    full_width = q_local * lax.axis_size("tp")
    q_scale = lax.rsqrt(square_sums[0] / full_width + norm_epsilon)[:, None]
    k_scale = lax.rsqrt(square_sums[1] / full_width + norm_epsilon)[:, None]
    half_size = HD // 2
    positions = jnp.arange(seq_len).astype(jnp.float32)
    frequency = rope_theta ** (-jnp.arange(half_size).astype(jnp.float32) * 2.0 / HD)
    angles = positions[:, None] * frequency[None, :]
    cosine, sine = jnp.cos(angles), jnp.sin(angles)
    cos_full = jnp.concatenate([cosine, cosine], -1)
    sin_signed = jnp.concatenate([-sine, sine], -1)
    attended, k_flat, v_flat = fused_attention(
        projected, q_scale, k_scale, q_gain[None], k_gain[None], cos_full, sin_signed, lengths, req_dev, seq_len
    )
    attended = attended.reshape(req_dev, seq_len, q_local)
    page_count = seq_len // PAGE
    home_index = lax.axis_index(REQ)
    axis_count = lax.psum(1, REQ)
    is_live = (jnp.arange(page_count) * PAGE)[None, :] < lengths[:, None]
    offset = (page_holder - home_index + 1 + axis_count) % axis_count - 1
    target = jnp.where(is_live, (offset + 1) * CAP + page_slot, -1).reshape(-1)
    onehot = (target[None, :] == jnp.arange(SLOTS)[:, None]).astype(jnp.bfloat16)
    stacked = jnp.stack(
        [
            k_flat.reshape(req_dev * page_count, PAGE * q_local),
            v_flat.reshape(req_dev * page_count, PAGE * q_local),
        ],
        1,
    )
    stacked = stacked.reshape(req_dev * page_count, 2 * PAGE * q_local)
    outgoing = (
        jnp.dot(onehot, stacked, preferred_element_type=jnp.float32)
        .astype(jnp.bfloat16)
        .reshape(SLOTS, 2, PAGE, q_local)
    )
    padded = extended(outgoing, ((REQ, 0),), CAP)
    kv_cache = jnp.concatenate([padded[CAP + SLOTS :], outgoing[CAP : 2 * CAP], padded[:CAP]], 0)
    return (attended, kv_cache)


REQ = ("yh", "z", "x", "c")


def solution(mesh):
    fine = Mesh(np.asarray(mesh.devices).reshape(2, 8, 4, 2, mesh.shape["tp"]), REQ + ("tp",))
    in_specs = (
        P(REQ, None, None),
        P(REQ, None, "tp"),
        P("tp"),
        P("tp"),
        P(REQ),
        P(REQ, None),
        P(REQ, None),
    )
    out_specs = (P(REQ, None, "tp"), P(REQ, None, None, "tp"))
    return jax.shard_map(body, mesh=fine, in_specs=in_specs, out_specs=out_specs, check_vma=False)
```

```python
import jax
import jax.numpy as jnp
from jax import lax
from jax.experimental import pallas as pl
from jax.experimental.pallas import tpu as pltpu
import numpy as np
from jax.sharding import Mesh, PartitionSpec as P

HD = 128
PAGE = 128
CAP = 3
SLOTS = 9


norm_epsilon = 1e-06
rope_theta = 500000.0


def _put(out, piece, idx, at, col=0):
    starts = [0] * out.ndim
    starts[at] = idx
    starts[-1] = col
    return lax.dynamic_update_slice(out, jnp.expand_dims(piece, at), starts)

def ring_gather(x, axis, n, me, at=0):
    out = jnp.zeros(x.shape[:at] + (n,) + x.shape[at:], x.dtype)
    out = _put(out, x, me, at)
    if n == 2:
        other = lax.ppermute(x, axis, [(0, 1), (1, 0)])
        return _put(out, other, 1 - me, at)
    fwd = [(i, (i + 1) % n) for i in range(n)]
    bwd = [((i + 1) % n, i) for i in range(n)]
    left, right = x, x
    half = n // 2
    for s in range(1, (n + 1) // 2):
        left = lax.ppermute(left, axis, fwd)
        right = lax.ppermute(right, axis, bwd)
        out = _put(out, left, (me - s) % n, at)
        out = _put(out, right, (me + s) % n, at)
    if n % 2 == 0:
        h = x.shape[-1] // 2
        a = lax.ppermute(left[..., :h], axis, fwd)
        b = lax.ppermute(right[..., h:], axis, bwd)
        j = (me + half) % n
        out = _put(out, a, j, at, 0)
        out = _put(out, b, j, at, h)
    return out

def weight_gather(b):
    yh, z, x = (lax.axis_index(a) for a in ("yh", "z", "x"))
    g = ring_gather(b, "yh", 2, yh)
    ga = ring_gather(g[0], "x", 4, x)
    ga = ring_gather(ga, "z", 8, z)
    gb = ring_gather(g[1], "z", 8, z)
    gb = ring_gather(gb, "x", 4, x, at=1)
    return ga, gb


def project(token_rows, master_local):
    n, width = token_rows.shape
    cols = master_local.shape[-1]
    c = lax.axis_index("c")
    ga, gb = weight_gather(master_local)
    pieces = (ga, gb)
    swapped = tuple(lax.ppermute(p, "c", [(0, 1), (1, 0)]) for p in pieces)
    per_block = master_local.shape[0]
    t5 = token_rows.reshape(n, 2, width // (4 * per_block), 2, per_block)

    def columns(yh_index, c_index):
        part = lax.dynamic_slice(t5, (0, yh_index, 0, c_index, 0), (n, 1, t5.shape[2], 1, per_block))
        return part.reshape(n, -1)

    total = None
    for core, group in ((c, pieces), (1 - c, swapped)):
        for yh_index, piece in enumerate(group):
            term = jnp.dot(columns(yh_index, core), piece.reshape(-1, cols), preferred_element_type=jnp.float32)
            total = term if total is None else total + term
    return total


def rope_kernel(q_ref, k_ref, v_ref, rq_ref, rk_ref, gq_ref, gk_ref, cos_ref, sin_ref, qrot_ref, krot_ref, vout_ref):
    cos = cos_ref[...]
    sin = sin_ref[...]
    q = q_ref[...] * rq_ref[...] * gq_ref[...]
    k = k_ref[...] * rk_ref[...] * gk_ref[...]
    qrot_ref[...] = (q * cos + pltpu.roll(q, HD // 2, 1) * sin).astype(jnp.bfloat16)
    krot_ref[...] = (k * cos + pltpu.roll(k, HD // 2, 1) * sin).astype(jnp.bfloat16)
    vout_ref[...] = v_ref[...].astype(jnp.bfloat16)


def attn_kernel(len_ref, q_ref, k_ref, v_ref, att_ref):
    length = len_ref[pl.program_id(0)]
    seq = q_ref.shape[0]
    scores = lax.dot_general(q_ref[...], k_ref[...], (((1,), (1,)), ((), ())),
                             preferred_element_type=jnp.float32) * HD ** (-0.5)
    t = lax.broadcasted_iota(jnp.int32, (seq, seq), 0)
    u = lax.broadcasted_iota(jnp.int32, (seq, seq), 1)
    allowed = (u <= t) & (u < length)
    scores = jnp.where(allowed, scores, -1e30)
    row_max = jnp.max(scores, axis=-1, keepdims=True)
    exp_terms = jnp.where(allowed, jnp.exp(scores - row_max), 0.0)
    probs = (exp_terms / jnp.sum(exp_terms, axis=-1, keepdims=True)).astype(jnp.bfloat16)
    out = jnp.dot(probs, v_ref[...], preferred_element_type=jnp.float32)
    rows = lax.broadcasted_iota(jnp.int32, (seq, 1), 0)
    att_ref[...] = jnp.where(rows < length, out, 0.0).astype(jnp.bfloat16)


def rope_and_round(projected, rq, rk, q_gain, k_gain, cos_full, sin_signed, req_dev, seq):
    q_local = projected.shape[1] // 3
    heads = q_local // HD
    blk = lambda off: pl.BlockSpec((seq, HD), lambda r, h: (r, off + h))
    row = pl.BlockSpec((seq, 1), lambda r, h: (r, 0))
    gain = pl.BlockSpec((1, HD), lambda r, h: (0, h))
    table = pl.BlockSpec((seq, HD), lambda r, h: (0, 0))
    out = pl.BlockSpec((seq, HD), lambda r, h: (r, h))
    shape = jax.ShapeDtypeStruct((req_dev * seq, q_local), jnp.bfloat16)
    steps = req_dev * heads
    cost = pl.CostEstimate(flops=steps * seq * HD * 12, transcendentals=0,
                           bytes_accessed=steps * seq * HD * (3 * 4 + 3 * 2))
    return pl.pallas_call(
        rope_kernel,
        grid=(req_dev, heads),
        in_specs=[blk(0), blk(heads), blk(2 * heads), row, row, gain, gain, table, table],
        out_specs=[out, out, out],
        out_shape=[shape, shape, shape],
        cost_estimate=cost,
        name="rope_and_round",
    )(projected, projected, projected, rq, rk, q_gain, k_gain, cos_full, sin_signed)


def causal_attention(q_rot, k_rot, vals, lengths, req_dev, seq):
    q_local = q_rot.shape[1]
    heads = q_local // HD
    blk = pl.BlockSpec((seq, HD), lambda r, h, L: (r, h))
    steps = req_dev * heads
    cost = pl.CostEstimate(flops=steps * 4 * seq * seq * HD, transcendentals=steps * seq * seq,
                           bytes_accessed=steps * seq * HD * 2 * 4)
    return pl.pallas_call(
        attn_kernel,
        grid_spec=pltpu.PrefetchScalarGridSpec(
            num_scalar_prefetch=1, grid=(req_dev, heads), in_specs=[blk, blk, blk], out_specs=blk),
        out_shape=jax.ShapeDtypeStruct((req_dev * seq, q_local), jnp.bfloat16),
        cost_estimate=cost,
        name="causal_attention",
    )(lengths, q_rot, k_rot, vals)


def extended(block, sides, width):
    for axis, dim in sides:
        count = lax.psum(1, axis)
        forward = [(i, i + 1) for i in range(count - 1)]
        forward.append((count - 1, 0))
        backward = [(target, source) for source, target in forward]
        low = lax.ppermute(
            lax.slice_in_dim(block, block.shape[dim] - width, None, axis=dim), axis, forward
        )
        high = lax.ppermute(lax.slice_in_dim(block, 0, width, axis=dim), axis, backward)
        block = jnp.concatenate([low, block, high], axis=dim)
    return block


def rotate(values_in, seq_len, head_size):
    half_size = head_size // 2
    positions = jnp.arange(seq_len).astype(jnp.float32)
    frequency = rope_theta ** (-jnp.arange(half_size).astype(jnp.float32) * 2.0 / head_size)
    angles = positions[:, None] * frequency[None, :]
    cosine_table = jnp.cos(angles)[:, None, :]
    sine_table = jnp.sin(angles)[:, None, :]
    front_half = values_in[..., :half_size]
    back_half = values_in[..., half_size:]
    return jnp.concatenate(
        [
            front_half * cosine_table - back_half * sine_table,
            back_half * cosine_table + front_half * sine_table,
        ],
        -1,
    )


def attend(request_item):
    queries, key_rows, value_rows, length = request_item
    seq_len = queries.shape[0]
    scores = jnp.einsum(
        "thd,uhd->htu", queries, key_rows, preferred_element_type=jnp.float32
    ) * HD ** (-0.5)
    query_pos = jnp.arange(seq_len)[:, None]
    key_pos = jnp.arange(seq_len)[None, :]
    allowed = (key_pos <= query_pos) & (key_pos < length)
    scores = jnp.where(allowed[None], scores, -1e30)
    row_max = jnp.max(scores, axis=-1, keepdims=True)
    exp_terms = jnp.where(allowed[None], jnp.exp(scores - row_max), 0.0)
    probs = (exp_terms / jnp.sum(exp_terms, axis=-1, keepdims=True)).astype(jnp.bfloat16)
    output = jnp.einsum("htu,uhd->thd", probs, value_rows, preferred_element_type=jnp.float32)
    keep_rows = jnp.arange(seq_len)[:, None, None] < length
    return jnp.where(keep_rows, output, 0.0).astype(jnp.bfloat16)


def body(tokens, qkv_master, q_gain, k_gain, lengths, page_holder, page_slot):
    req_dev, seq_len, model_width = tokens.shape
    row_share, _, q_local = qkv_master.shape
    heads_local = q_local // HD
    token_rows = tokens.reshape(req_dev * seq_len, model_width)
    master_local = qkv_master.astype(jnp.bfloat16).reshape(row_share, 3 * q_local)
    projected = project(token_rows, master_local)
    square_sums = lax.psum(
        (
            jnp.sum(projected[:, :q_local] * projected[:, :q_local], -1),
            jnp.sum(projected[:, q_local : 2 * q_local] * projected[:, q_local : 2 * q_local], -1),
        ),
        "tp",
    )
    full_width = q_local * lax.axis_size("tp")
    q_scale = lax.rsqrt(square_sums[0] / full_width + norm_epsilon)[:, None]
    k_scale = lax.rsqrt(square_sums[1] / full_width + norm_epsilon)[:, None]
    half_size = HD // 2
    positions = jnp.arange(seq_len).astype(jnp.float32)
    frequency = rope_theta ** (-jnp.arange(half_size).astype(jnp.float32) * 2.0 / HD)
    angles = positions[:, None] * frequency[None, :]
    cosine, sine = jnp.cos(angles), jnp.sin(angles)
    cos_full = jnp.concatenate([cosine, cosine], -1)
    sin_signed = jnp.concatenate([-sine, sine], -1)
    q_flat, k_flat, v_flat = rope_and_round(
        projected, q_scale, k_scale, q_gain[None], k_gain[None], cos_full, sin_signed, req_dev, seq_len
    )
    attended = causal_attention(q_flat, k_flat, v_flat, lengths, req_dev, seq_len)
    attended = attended.reshape(req_dev, seq_len, q_local)
    page_count = seq_len // PAGE
    home_index = lax.axis_index(REQ)
    axis_count = lax.psum(1, REQ)
    is_live = (jnp.arange(page_count) * PAGE)[None, :] < lengths[:, None]
    offset = (page_holder - home_index + 1 + axis_count) % axis_count - 1
    target = jnp.where(is_live, (offset + 1) * CAP + page_slot, -1).reshape(-1)
    onehot = (target[None, :] == jnp.arange(SLOTS)[:, None]).astype(jnp.bfloat16)
    stacked = jnp.stack(
        [
            k_flat.reshape(req_dev * page_count, PAGE * q_local),
            v_flat.reshape(req_dev * page_count, PAGE * q_local),
        ],
        1,
    )
    stacked = stacked.reshape(req_dev * page_count, 2 * PAGE * q_local)
    outgoing = (
        jnp.dot(onehot, stacked, preferred_element_type=jnp.float32)
        .astype(jnp.bfloat16)
        .reshape(SLOTS, 2, PAGE, q_local)
    )
    padded = extended(outgoing, ((REQ, 0),), CAP)
    kv_cache = jnp.concatenate([padded[CAP + SLOTS :], outgoing[CAP : 2 * CAP], padded[:CAP]], 0)
    return (attended, kv_cache)


REQ = ("yh", "z", "x", "c")


def solution(mesh):
    fine = Mesh(np.asarray(mesh.devices).reshape(2, 8, 4, 2, mesh.shape["tp"]), REQ + ("tp",))
    in_specs = (
        P(REQ, None, None),
        P(REQ, None, "tp"),
        P("tp"),
        P("tp"),
        P(REQ),
        P(REQ, None),
        P(REQ, None),
    )
    out_specs = (P(REQ, None, "tp"), P(REQ, None, None, "tp"))
    return jax.shard_map(body, mesh=fine, in_specs=in_specs, out_specs=out_specs, check_vma=False)
```

```python
import jax
import jax.numpy as jnp
from jax import lax
from jax.experimental import pallas as pl
from jax.experimental.pallas import tpu as pltpu
import numpy as np
from jax.sharding import Mesh, PartitionSpec as P

HD = 128
ROPE_WIDTH = 512
PAGE = 128
CAP = 3
SLOTS = 9


norm_epsilon = 1e-06
rope_theta = 500000.0


def _put(out, piece, idx, at, col=0):
    starts = [0] * out.ndim
    starts[at] = idx
    starts[-1] = col
    return lax.dynamic_update_slice(out, jnp.expand_dims(piece, at), starts)

def ring_gather(x, axis, n, me, at=0):
    out = jnp.zeros(x.shape[:at] + (n,) + x.shape[at:], x.dtype)
    out = _put(out, x, me, at)
    if n == 2:
        other = lax.ppermute(x, axis, [(0, 1), (1, 0)])
        return _put(out, other, 1 - me, at)
    fwd = [(i, (i + 1) % n) for i in range(n)]
    bwd = [((i + 1) % n, i) for i in range(n)]
    left, right = x, x
    half = n // 2
    for s in range(1, (n + 1) // 2):
        left = lax.ppermute(left, axis, fwd)
        right = lax.ppermute(right, axis, bwd)
        out = _put(out, left, (me - s) % n, at)
        out = _put(out, right, (me + s) % n, at)
    if n % 2 == 0:
        h = x.shape[-1] // 2
        a = lax.ppermute(left[..., :h], axis, fwd)
        b = lax.ppermute(right[..., h:], axis, bwd)
        j = (me + half) % n
        out = _put(out, a, j, at, 0)
        out = _put(out, b, j, at, h)
    return out

def weight_gather(b):
    yh, z, x, c = (lax.axis_index(a) for a in ("yh", "z", "x", "c"))
    g = ring_gather(b, "yh", 2, yh)
    ga = ring_gather(g[0], "x", 4, x)
    ga = ring_gather(ga, "z", 8, z)
    gb = ring_gather(g[1], "z", 8, z)
    gb = ring_gather(gb, "x", 4, x, at=1)
    own = jnp.stack([ga, gb])
    return ring_gather(own, "c", 2, c, at=3)


def rope_kernel(q_ref, k_ref, v_ref, rq_ref, rk_ref, gq_ref, gk_ref, cos_ref, sin_ref, qrot_ref, krot_ref, vout_ref):
    cos = cos_ref[...]
    sin = sin_ref[...]
    width = cos.shape[1]
    lane = lax.broadcasted_iota(jnp.int32, cos.shape, 1)
    partner = jnp.where(lane % HD < HD // 2, lane + HD // 2, lane - HD // 2)
    from_first = pltpu.roll(lane, HD // 2, 1) == partner

    def rotated(x):
        swapped = jnp.where(from_first, pltpu.roll(x, HD // 2, 1), pltpu.roll(x, width - HD // 2, 1))
        return x * cos + swapped * sin

    q = q_ref[...] * rq_ref[...] * gq_ref[...]
    k = k_ref[...] * rk_ref[...] * gk_ref[...]
    qrot_ref[...] = rotated(q).astype(jnp.bfloat16)
    krot_ref[...] = rotated(k).astype(jnp.bfloat16)
    vout_ref[...] = v_ref[...].astype(jnp.bfloat16)


def attn_kernel(len_ref, q_ref, k_ref, v_ref, att_ref):
    length = len_ref[pl.program_id(0)]
    seq = q_ref.shape[0]
    scores = lax.dot_general(q_ref[...], k_ref[...], (((1,), (1,)), ((), ())),
                             preferred_element_type=jnp.float32) * HD ** (-0.5)
    t = lax.broadcasted_iota(jnp.int32, (seq, seq), 0)
    u = lax.broadcasted_iota(jnp.int32, (seq, seq), 1)
    allowed = (u <= t) & (u < length)
    scores = jnp.where(allowed, scores, -1e30)
    row_max = jnp.max(scores, axis=-1, keepdims=True)
    exp_terms = jnp.where(allowed, jnp.exp(scores - row_max), 0.0)
    probs = (exp_terms / jnp.sum(exp_terms, axis=-1, keepdims=True)).astype(jnp.bfloat16)
    out = jnp.dot(probs, v_ref[...], preferred_element_type=jnp.float32)
    rows = lax.broadcasted_iota(jnp.int32, (seq, 1), 0)
    att_ref[...] = jnp.where(rows < length, out, 0.0).astype(jnp.bfloat16)


def rope_and_round(projected, rq, rk, q_gain, k_gain, cos_full, sin_signed, req_dev, seq):
    q_local = projected.shape[1] // 3
    width = ROPE_WIDTH if q_local % ROPE_WIDTH == 0 else HD
    groups = q_local // width
    blk = lambda off: pl.BlockSpec((seq, width), lambda r, h: (r, off + h))
    row = pl.BlockSpec((seq, 1), lambda r, h: (r, 0))
    gain = pl.BlockSpec((1, width), lambda r, h: (0, h))
    table = pl.BlockSpec((seq, width), lambda r, h: (0, 0))
    out = pl.BlockSpec((seq, width), lambda r, h: (r, h))
    shape = jax.ShapeDtypeStruct((req_dev * seq, q_local), jnp.bfloat16)
    reps = width // HD
    cos_full = jnp.tile(cos_full, (1, reps))
    sin_signed = jnp.tile(sin_signed, (1, reps))
    steps = req_dev * groups
    cost = pl.CostEstimate(flops=steps * seq * width * 12, transcendentals=0,
                           bytes_accessed=steps * seq * width * (3 * 4 + 3 * 2))
    return pl.pallas_call(
        rope_kernel,
        grid=(req_dev, groups),
        in_specs=[blk(0), blk(groups), blk(2 * groups), row, row, gain, gain, table, table],
        out_specs=[out, out, out],
        out_shape=[shape, shape, shape],
        cost_estimate=cost,
        name="rope_and_round",
    )(projected, projected, projected, rq, rk, q_gain, k_gain, cos_full, sin_signed)


def causal_attention(q_rot, k_rot, vals, lengths, req_dev, seq):
    q_local = q_rot.shape[1]
    heads = q_local // HD
    blk = pl.BlockSpec((seq, HD), lambda r, h, L: (r, h))
    steps = req_dev * heads
    cost = pl.CostEstimate(flops=steps * 4 * seq * seq * HD, transcendentals=steps * seq * seq,
                           bytes_accessed=steps * seq * HD * 2 * 4)
    return pl.pallas_call(
        attn_kernel,
        grid_spec=pltpu.PrefetchScalarGridSpec(
            num_scalar_prefetch=1, grid=(req_dev, heads), in_specs=[blk, blk, blk], out_specs=blk),
        out_shape=jax.ShapeDtypeStruct((req_dev * seq, q_local), jnp.bfloat16),
        cost_estimate=cost,
        name="causal_attention",
    )(lengths, q_rot, k_rot, vals)


def extended(block, sides, width):
    for axis, dim in sides:
        count = lax.psum(1, axis)
        forward = [(i, i + 1) for i in range(count - 1)]
        forward.append((count - 1, 0))
        backward = [(target, source) for source, target in forward]
        low = lax.ppermute(
            lax.slice_in_dim(block, block.shape[dim] - width, None, axis=dim), axis, forward
        )
        high = lax.ppermute(lax.slice_in_dim(block, 0, width, axis=dim), axis, backward)
        block = jnp.concatenate([low, block, high], axis=dim)
    return block


def rotate(values_in, seq_len, head_size):
    half_size = head_size // 2
    positions = jnp.arange(seq_len).astype(jnp.float32)
    frequency = rope_theta ** (-jnp.arange(half_size).astype(jnp.float32) * 2.0 / head_size)
    angles = positions[:, None] * frequency[None, :]
    cosine_table = jnp.cos(angles)[:, None, :]
    sine_table = jnp.sin(angles)[:, None, :]
    front_half = values_in[..., :half_size]
    back_half = values_in[..., half_size:]
    return jnp.concatenate(
        [
            front_half * cosine_table - back_half * sine_table,
            back_half * cosine_table + front_half * sine_table,
        ],
        -1,
    )


def attend(request_item):
    queries, key_rows, value_rows, length = request_item
    seq_len = queries.shape[0]
    scores = jnp.einsum(
        "thd,uhd->htu", queries, key_rows, preferred_element_type=jnp.float32
    ) * HD ** (-0.5)
    query_pos = jnp.arange(seq_len)[:, None]
    key_pos = jnp.arange(seq_len)[None, :]
    allowed = (key_pos <= query_pos) & (key_pos < length)
    scores = jnp.where(allowed[None], scores, -1e30)
    row_max = jnp.max(scores, axis=-1, keepdims=True)
    exp_terms = jnp.where(allowed[None], jnp.exp(scores - row_max), 0.0)
    probs = (exp_terms / jnp.sum(exp_terms, axis=-1, keepdims=True)).astype(jnp.bfloat16)
    output = jnp.einsum("htu,uhd->thd", probs, value_rows, preferred_element_type=jnp.float32)
    keep_rows = jnp.arange(seq_len)[:, None, None] < length
    return jnp.where(keep_rows, output, 0.0).astype(jnp.bfloat16)


def body(tokens, qkv_master, q_gain, k_gain, lengths, page_holder, page_slot):
    req_dev, seq_len, model_width = tokens.shape
    row_share, _, q_local = qkv_master.shape
    heads_local = q_local // HD
    token_rows = tokens.reshape(req_dev * seq_len, model_width)
    master_local = qkv_master.astype(jnp.bfloat16).reshape(row_share, 3 * q_local)
    gathered = weight_gather(master_local).reshape(-1, master_local.shape[-1])
    projected = jnp.dot(token_rows, gathered, preferred_element_type=jnp.float32)
    square_sums = lax.psum(
        (
            jnp.sum(projected[:, :q_local] * projected[:, :q_local], -1),
            jnp.sum(projected[:, q_local : 2 * q_local] * projected[:, q_local : 2 * q_local], -1),
        ),
        "tp",
    )
    full_width = q_local * lax.axis_size("tp")
    q_scale = lax.rsqrt(square_sums[0] / full_width + norm_epsilon)[:, None]
    k_scale = lax.rsqrt(square_sums[1] / full_width + norm_epsilon)[:, None]
    half_size = HD // 2
    positions = jnp.arange(seq_len).astype(jnp.float32)
    frequency = rope_theta ** (-jnp.arange(half_size).astype(jnp.float32) * 2.0 / HD)
    angles = positions[:, None] * frequency[None, :]
    cosine, sine = jnp.cos(angles), jnp.sin(angles)
    cos_full = jnp.concatenate([cosine, cosine], -1)
    sin_signed = jnp.concatenate([-sine, sine], -1)
    q_flat, k_flat, v_flat = rope_and_round(
        projected, q_scale, k_scale, q_gain[None], k_gain[None], cos_full, sin_signed, req_dev, seq_len
    )
    attended = causal_attention(q_flat, k_flat, v_flat, lengths, req_dev, seq_len)
    attended = attended.reshape(req_dev, seq_len, q_local)
    page_count = seq_len // PAGE
    home_index = lax.axis_index(REQ)
    axis_count = lax.psum(1, REQ)
    is_live = (jnp.arange(page_count) * PAGE)[None, :] < lengths[:, None]
    offset = (page_holder - home_index + 1 + axis_count) % axis_count - 1
    target = jnp.where(is_live, (offset + 1) * CAP + page_slot, -1).reshape(-1)
    onehot = (target[None, :] == jnp.arange(SLOTS)[:, None]).astype(jnp.bfloat16)
    stacked = jnp.stack(
        [
            k_flat.reshape(req_dev * page_count, PAGE * q_local),
            v_flat.reshape(req_dev * page_count, PAGE * q_local),
        ],
        1,
    )
    stacked = stacked.reshape(req_dev * page_count, 2 * PAGE * q_local)
    outgoing = (
        jnp.dot(onehot, stacked, preferred_element_type=jnp.float32)
        .astype(jnp.bfloat16)
        .reshape(SLOTS, 2, PAGE, q_local)
    )
    padded = extended(outgoing, ((REQ, 0),), CAP)
    kv_cache = jnp.concatenate([padded[CAP + SLOTS :], outgoing[CAP : 2 * CAP], padded[:CAP]], 0)
    return (attended, kv_cache)


REQ = ("yh", "z", "x", "c")


def solution(mesh):
    fine = Mesh(np.asarray(mesh.devices).reshape(2, 8, 4, 2, mesh.shape["tp"]), REQ + ("tp",))
    in_specs = (
        P(REQ, None, None),
        P(REQ, None, "tp"),
        P("tp"),
        P("tp"),
        P(REQ),
        P(REQ, None),
        P(REQ, None),
    )
    out_specs = (P(REQ, None, "tp"), P(REQ, None, None, "tp"))
    return jax.shard_map(body, mesh=fine, in_specs=in_specs, out_specs=out_specs, check_vma=False)
```

```python
import jax
import jax.numpy as jnp
from jax import lax
from jax.experimental import pallas as pl
from jax.experimental.pallas import tpu as pltpu
import numpy as np
from jax.sharding import Mesh, PartitionSpec as P

HD = 128
ROPE_WIDTH = 512
PAGE = 128
CAP = 3
SLOTS = 9


norm_epsilon = 1e-06
rope_theta = 500000.0


def _put(out, piece, idx, at, col=0):
    starts = [0] * out.ndim
    starts[at] = idx
    starts[-1] = col
    return lax.dynamic_update_slice(out, jnp.expand_dims(piece, at), starts)

def ring_gather(x, axis, n, me, at=0):
    out = jnp.zeros(x.shape[:at] + (n,) + x.shape[at:], x.dtype)
    out = _put(out, x, me, at)
    if n == 2:
        other = lax.ppermute(x, axis, [(0, 1), (1, 0)])
        return _put(out, other, 1 - me, at)
    fwd = [(i, (i + 1) % n) for i in range(n)]
    bwd = [((i + 1) % n, i) for i in range(n)]
    left, right = x, x
    half = n // 2
    for s in range(1, (n + 1) // 2):
        left = lax.ppermute(left, axis, fwd)
        right = lax.ppermute(right, axis, bwd)
        out = _put(out, left, (me - s) % n, at)
        out = _put(out, right, (me + s) % n, at)
    if n % 2 == 0:
        h = x.shape[-1] // 2
        a = lax.ppermute(left[..., :h], axis, fwd)
        b = lax.ppermute(right[..., h:], axis, bwd)
        j = (me + half) % n
        out = _put(out, a, j, at, 0)
        out = _put(out, b, j, at, h)
    return out

def weight_gather(b):
    yh, z, x = (lax.axis_index(a) for a in ("yh", "z", "x"))
    g = ring_gather(b, "yh", 2, yh)
    ga = ring_gather(g[0], "x", 4, x)
    ga = ring_gather(ga, "z", 8, z)
    gb = ring_gather(g[1], "z", 8, z)
    gb = ring_gather(gb, "x", 4, x, at=1)
    return ga, gb


def project(token_rows, master_local):
    n, width = token_rows.shape
    per_block, cols = master_local.shape
    c = lax.axis_index("c")
    ga, gb = weight_gather(master_local)
    swap = [(0, 1), (1, 0)]
    weight = jnp.stack([jnp.stack([ga, gb]), jnp.stack([lax.ppermute(ga, "c", swap), lax.ppermute(gb, "c", swap)])])
    t = token_rows.reshape(n, 2, width // (4 * per_block), 2, per_block)
    t = jnp.where(c == 0, t, jnp.flip(t, 3))
    t = jnp.transpose(t, (0, 3, 1, 2, 4)).reshape(n, width)
    return jnp.dot(t, weight.reshape(-1, cols), preferred_element_type=jnp.float32)


def rope_kernel(q_ref, k_ref, v_ref, rq_ref, rk_ref, gq_ref, gk_ref, cos_ref, sin_ref, qrot_ref, kv_ref):
    cos = cos_ref[...]
    sin = sin_ref[...]
    width = cos.shape[1]
    lane = lax.broadcasted_iota(jnp.int32, cos.shape, 1)
    partner = jnp.where(lane % HD < HD // 2, lane + HD // 2, lane - HD // 2)
    from_first = pltpu.roll(lane, HD // 2, 1) == partner

    def rotated(x):
        swapped = jnp.where(from_first, pltpu.roll(x, HD // 2, 1), pltpu.roll(x, width - HD // 2, 1))
        return x * cos + swapped * sin

    q = q_ref[...] * rq_ref[...] * gq_ref[...]
    k = k_ref[...] * rk_ref[...] * gk_ref[...]
    qrot_ref[...] = rotated(q).astype(jnp.bfloat16)
    pages = kv_ref.shape[0]
    kv_ref[:, 0, :, :] = rotated(k).astype(jnp.bfloat16).reshape(pages, -1, width)
    kv_ref[:, 1, :, :] = v_ref[...].astype(jnp.bfloat16).reshape(pages, -1, width)


def attn_kernel(len_ref, q_ref, k_ref, v_ref, att_ref):
    length = len_ref[pl.program_id(0)]
    seq = q_ref.shape[0]
    keys = k_ref[...].reshape(seq, -1)
    vals = v_ref[...].reshape(seq, -1)
    scores = lax.dot_general(q_ref[...], keys, (((1,), (1,)), ((), ())),
                             preferred_element_type=jnp.float32) * HD ** (-0.5)
    t = lax.broadcasted_iota(jnp.int32, (seq, seq), 0)
    u = lax.broadcasted_iota(jnp.int32, (seq, seq), 1)
    allowed = (u <= t) & (u < length)
    scores = jnp.where(allowed, scores, -1e30)
    row_max = jnp.max(scores, axis=-1, keepdims=True)
    exp_terms = jnp.where(allowed, jnp.exp(scores - row_max), 0.0)
    probs = (exp_terms / jnp.sum(exp_terms, axis=-1, keepdims=True)).astype(jnp.bfloat16)
    out = jnp.dot(probs, vals, preferred_element_type=jnp.float32)
    rows = lax.broadcasted_iota(jnp.int32, (seq, 1), 0)
    att_ref[...] = jnp.where(rows < length, out, 0.0).astype(jnp.bfloat16)


def rope_and_round(projected, rq, rk, q_gain, k_gain, cos_full, sin_signed, req_dev, seq):
    q_local = projected.shape[1] // 3
    width = ROPE_WIDTH if q_local % ROPE_WIDTH == 0 else HD
    groups = q_local // width
    blk = lambda off: pl.BlockSpec((seq, width), lambda r, h: (r, off + h))
    row = pl.BlockSpec((seq, 1), lambda r, h: (r, 0))
    gain = pl.BlockSpec((1, width), lambda r, h: (0, h))
    table = pl.BlockSpec((seq, width), lambda r, h: (0, 0))
    out = pl.BlockSpec((seq, width), lambda r, h: (r, h))
    pages = seq // PAGE
    kv_out = pl.BlockSpec((pages, 2, PAGE, width), lambda r, h: (r, 0, 0, h))
    shape = jax.ShapeDtypeStruct((req_dev * seq, q_local), jnp.bfloat16)
    kv_shape = jax.ShapeDtypeStruct((req_dev * pages, 2, PAGE, q_local), jnp.bfloat16)
    reps = width // HD
    cos_full = jnp.tile(cos_full, (1, reps))
    sin_signed = jnp.tile(sin_signed, (1, reps))
    steps = req_dev * groups
    cost = pl.CostEstimate(flops=steps * seq * width * 12, transcendentals=0,
                           bytes_accessed=steps * seq * width * (3 * 4 + 3 * 2))
    return pl.pallas_call(
        rope_kernel,
        grid=(req_dev, groups),
        in_specs=[blk(0), blk(groups), blk(2 * groups), row, row, gain, gain, table, table],
        out_specs=[out, kv_out],
        out_shape=[shape, kv_shape],
        cost_estimate=cost,
        name="rope_and_round",
    )(projected, projected, projected, rq, rk, q_gain, k_gain, cos_full, sin_signed)


def causal_attention(q_rot, kv_pages, lengths, req_dev, seq):
    q_local = q_rot.shape[1]
    heads = q_local // HD
    pages = seq // PAGE
    blk = pl.BlockSpec((seq, HD), lambda r, h, L: (r, h))
    page_blk = lambda which: pl.BlockSpec((pages, None, PAGE, HD), lambda r, h, L: (r, which, 0, h))
    steps = req_dev * heads
    cost = pl.CostEstimate(flops=steps * 4 * seq * seq * HD, transcendentals=steps * seq * seq,
                           bytes_accessed=steps * seq * HD * 2 * 4)
    return pl.pallas_call(
        attn_kernel,
        grid_spec=pltpu.PrefetchScalarGridSpec(
            num_scalar_prefetch=1, grid=(req_dev, heads), in_specs=[blk, page_blk(0), page_blk(1)], out_specs=blk),
        out_shape=jax.ShapeDtypeStruct((req_dev * seq, q_local), jnp.bfloat16),
        cost_estimate=cost,
        name="causal_attention",
    )(lengths, q_rot, kv_pages, kv_pages)


def extended(block, sides, width):
    for axis, dim in sides:
        count = lax.psum(1, axis)
        forward = [(i, i + 1) for i in range(count - 1)]
        forward.append((count - 1, 0))
        backward = [(target, source) for source, target in forward]
        low = lax.ppermute(
            lax.slice_in_dim(block, block.shape[dim] - width, None, axis=dim), axis, forward
        )
        high = lax.ppermute(lax.slice_in_dim(block, 0, width, axis=dim), axis, backward)
        block = jnp.concatenate([low, block, high], axis=dim)
    return block


def rotate(values_in, seq_len, head_size):
    half_size = head_size // 2
    positions = jnp.arange(seq_len).astype(jnp.float32)
    frequency = rope_theta ** (-jnp.arange(half_size).astype(jnp.float32) * 2.0 / head_size)
    angles = positions[:, None] * frequency[None, :]
    cosine_table = jnp.cos(angles)[:, None, :]
    sine_table = jnp.sin(angles)[:, None, :]
    front_half = values_in[..., :half_size]
    back_half = values_in[..., half_size:]
    return jnp.concatenate(
        [
            front_half * cosine_table - back_half * sine_table,
            back_half * cosine_table + front_half * sine_table,
        ],
        -1,
    )


def attend(request_item):
    queries, key_rows, value_rows, length = request_item
    seq_len = queries.shape[0]
    scores = jnp.einsum(
        "thd,uhd->htu", queries, key_rows, preferred_element_type=jnp.float32
    ) * HD ** (-0.5)
    query_pos = jnp.arange(seq_len)[:, None]
    key_pos = jnp.arange(seq_len)[None, :]
    allowed = (key_pos <= query_pos) & (key_pos < length)
    scores = jnp.where(allowed[None], scores, -1e30)
    row_max = jnp.max(scores, axis=-1, keepdims=True)
    exp_terms = jnp.where(allowed[None], jnp.exp(scores - row_max), 0.0)
    probs = (exp_terms / jnp.sum(exp_terms, axis=-1, keepdims=True)).astype(jnp.bfloat16)
    output = jnp.einsum("htu,uhd->thd", probs, value_rows, preferred_element_type=jnp.float32)
    keep_rows = jnp.arange(seq_len)[:, None, None] < length
    return jnp.where(keep_rows, output, 0.0).astype(jnp.bfloat16)


def body(tokens, qkv_master, q_gain, k_gain, lengths, page_holder, page_slot):
    req_dev, seq_len, model_width = tokens.shape
    row_share, _, q_local = qkv_master.shape
    heads_local = q_local // HD
    token_rows = tokens.reshape(req_dev * seq_len, model_width)
    master_local = qkv_master.astype(jnp.bfloat16).reshape(row_share, 3 * q_local)
    projected = project(token_rows, master_local)
    square_sums = lax.psum(
        (
            jnp.sum(projected[:, :q_local] * projected[:, :q_local], -1),
            jnp.sum(projected[:, q_local : 2 * q_local] * projected[:, q_local : 2 * q_local], -1),
        ),
        "tp",
    )
    full_width = q_local * lax.axis_size("tp")
    q_scale = lax.rsqrt(square_sums[0] / full_width + norm_epsilon)[:, None]
    k_scale = lax.rsqrt(square_sums[1] / full_width + norm_epsilon)[:, None]
    half_size = HD // 2
    positions = jnp.arange(seq_len).astype(jnp.float32)
    frequency = rope_theta ** (-jnp.arange(half_size).astype(jnp.float32) * 2.0 / HD)
    angles = positions[:, None] * frequency[None, :]
    cosine, sine = jnp.cos(angles), jnp.sin(angles)
    cos_full = jnp.concatenate([cosine, cosine], -1)
    sin_signed = jnp.concatenate([-sine, sine], -1)
    q_flat, kv_pages = rope_and_round(
        projected, q_scale, k_scale, q_gain[None], k_gain[None], cos_full, sin_signed, req_dev, seq_len
    )
    attended = causal_attention(q_flat, kv_pages, lengths, req_dev, seq_len)
    attended = attended.reshape(req_dev, seq_len, q_local)
    page_count = seq_len // PAGE
    home_index = lax.axis_index(REQ)
    axis_count = lax.psum(1, REQ)
    is_live = (jnp.arange(page_count) * PAGE)[None, :] < lengths[:, None]
    offset = (page_holder - home_index + 1 + axis_count) % axis_count - 1
    target = jnp.where(is_live, (offset + 1) * CAP + page_slot, -1).reshape(-1)
    onehot = (target[None, :] == jnp.arange(SLOTS)[:, None]).astype(jnp.bfloat16)
    stacked = kv_pages.reshape(req_dev * page_count, 2 * PAGE * q_local)
    outgoing = (
        jnp.dot(onehot, stacked, preferred_element_type=jnp.float32)
        .astype(jnp.bfloat16)
        .reshape(SLOTS, 2, PAGE, q_local)
    )
    padded = extended(outgoing, ((REQ, 0),), CAP)
    kv_cache = jnp.concatenate([padded[CAP + SLOTS :], outgoing[CAP : 2 * CAP], padded[:CAP]], 0)
    return (attended, kv_cache)


REQ = ("yh", "z", "x", "c")


def solution(mesh):
    fine = Mesh(np.asarray(mesh.devices).reshape(2, 8, 4, 2, mesh.shape["tp"]), REQ + ("tp",))
    in_specs = (
        P(REQ, None, None),
        P(REQ, None, "tp"),
        P("tp"),
        P("tp"),
        P(REQ),
        P(REQ, None),
        P(REQ, None),
    )
    out_specs = (P(REQ, None, "tp"), P(REQ, None, None, "tp"))
    return jax.shard_map(body, mesh=fine, in_specs=in_specs, out_specs=out_specs, check_vma=False)
```

```python
import jax
import jax.numpy as jnp
from jax import lax
from jax.experimental import pallas as pl
from jax.experimental.pallas import tpu as pltpu
import numpy as np
from jax.sharding import Mesh, PartitionSpec as P

HD = 128
ROPE_WIDTH = 512
PAGE = 128
CAP = 3
SLOTS = 9


norm_epsilon = 1e-06
rope_theta = 500000.0


def _put(out, piece, idx, at, col=0):
    starts = [0] * out.ndim
    starts[at] = idx
    starts[-1] = col
    return lax.dynamic_update_slice(out, jnp.expand_dims(piece, at), starts)

def ring_gather(x, axis, n, me, at=0):
    if n == 2:
        other = lax.ppermute(x, axis, [(0, 1), (1, 0)])
        return jnp.where(me == 0, jnp.stack([x, other], axis=at), jnp.stack([other, x], axis=at))
    out = jnp.zeros(x.shape[:at] + (n,) + x.shape[at:], x.dtype)
    out = _put(out, x, me, at)
    fwd = [(i, (i + 1) % n) for i in range(n)]
    bwd = [((i + 1) % n, i) for i in range(n)]
    left, right = x, x
    half = n // 2
    for s in range(1, (n + 1) // 2):
        left = lax.ppermute(left, axis, fwd)
        right = lax.ppermute(right, axis, bwd)
        out = _put(out, left, (me - s) % n, at)
        out = _put(out, right, (me + s) % n, at)
    if n % 2 == 0:
        h = x.shape[-1] // 2
        a = lax.ppermute(left[..., :h], axis, fwd)
        b = lax.ppermute(right[..., h:], axis, bwd)
        j = (me + half) % n
        out = _put(out, a, j, at, 0)
        out = _put(out, b, j, at, h)
    return out

def weight_gather(b):
    yh, z, x, c = (lax.axis_index(a) for a in ("yh", "z", "x", "c"))
    g = ring_gather(b, "yh", 2, yh)
    ga = ring_gather(g[0], "x", 4, x)
    ga = ring_gather(ga, "z", 8, z)
    gb = ring_gather(g[1], "z", 8, z)
    gb = ring_gather(gb, "x", 4, x, at=1)
    own = jnp.stack([ga, gb])
    return ring_gather(own, "c", 2, c, at=3)


def rope_kernel(q_ref, k_ref, v_ref, rq_ref, rk_ref, gq_ref, gk_ref, cos_ref, sin_ref, qrot_ref, kv_ref):
    cos = cos_ref[...]
    sin = sin_ref[...]
    width = cos.shape[1]
    lane = lax.broadcasted_iota(jnp.int32, cos.shape, 1)
    partner = jnp.where(lane % HD < HD // 2, lane + HD // 2, lane - HD // 2)
    from_first = pltpu.roll(lane, HD // 2, 1) == partner

    def rotated(x):
        swapped = jnp.where(from_first, pltpu.roll(x, HD // 2, 1), pltpu.roll(x, width - HD // 2, 1))
        return x * cos + swapped * sin

    q = q_ref[...] * rq_ref[...] * gq_ref[...]
    k = k_ref[...] * rk_ref[...] * gk_ref[...]
    qrot_ref[...] = rotated(q).astype(jnp.bfloat16)
    pages = kv_ref.shape[0]
    kv_ref[:, 0, :, :] = rotated(k).astype(jnp.bfloat16).reshape(pages, -1, width)
    kv_ref[:, 1, :, :] = v_ref[...].astype(jnp.bfloat16).reshape(pages, -1, width)


def attn_kernel(len_ref, q_ref, k_ref, v_ref, att_ref):
    length = len_ref[pl.program_id(0)]
    seq = q_ref.shape[0]
    keys = k_ref[...].reshape(seq, -1)
    vals = v_ref[...].reshape(seq, -1)
    scores = lax.dot_general(q_ref[...], keys, (((1,), (1,)), ((), ())),
                             preferred_element_type=jnp.float32) * HD ** (-0.5)
    t = lax.broadcasted_iota(jnp.int32, (seq, seq), 0)
    u = lax.broadcasted_iota(jnp.int32, (seq, seq), 1)
    allowed = (u <= t) & (u < length)
    scores = jnp.where(allowed, scores, -1e30)
    row_max = jnp.max(scores, axis=-1, keepdims=True)
    exp_terms = jnp.where(allowed, jnp.exp(scores - row_max), 0.0)
    probs = (exp_terms / jnp.sum(exp_terms, axis=-1, keepdims=True)).astype(jnp.bfloat16)
    out = jnp.dot(probs, vals, preferred_element_type=jnp.float32)
    rows = lax.broadcasted_iota(jnp.int32, (seq, 1), 0)
    att_ref[...] = jnp.where(rows < length, out, 0.0).astype(jnp.bfloat16)


def rope_and_round(projected, rq, rk, q_gain, k_gain, cos_full, sin_signed, req_dev, seq):
    q_local = projected.shape[1] // 3
    width = ROPE_WIDTH if q_local % ROPE_WIDTH == 0 else HD
    groups = q_local // width
    blk = lambda off: pl.BlockSpec((seq, width), lambda r, h: (r, off + h))
    row = pl.BlockSpec((seq, 1), lambda r, h: (r, 0))
    gain = pl.BlockSpec((1, width), lambda r, h: (0, h))
    table = pl.BlockSpec((seq, width), lambda r, h: (0, 0))
    out = pl.BlockSpec((seq, width), lambda r, h: (r, h))
    pages = seq // PAGE
    kv_out = pl.BlockSpec((pages, 2, PAGE, width), lambda r, h: (r, 0, 0, h))
    shape = jax.ShapeDtypeStruct((req_dev * seq, q_local), jnp.bfloat16)
    kv_shape = jax.ShapeDtypeStruct((req_dev * pages, 2, PAGE, q_local), jnp.bfloat16)
    reps = width // HD
    cos_full = jnp.tile(cos_full, (1, reps))
    sin_signed = jnp.tile(sin_signed, (1, reps))
    steps = req_dev * groups
    cost = pl.CostEstimate(flops=steps * seq * width * 12, transcendentals=0,
                           bytes_accessed=steps * seq * width * (3 * 4 + 3 * 2))
    return pl.pallas_call(
        rope_kernel,
        grid=(req_dev, groups),
        in_specs=[blk(0), blk(groups), blk(2 * groups), row, row, gain, gain, table, table],
        out_specs=[out, kv_out],
        out_shape=[shape, kv_shape],
        cost_estimate=cost,
        name="rope_and_round",
    )(projected, projected, projected, rq, rk, q_gain, k_gain, cos_full, sin_signed)


def causal_attention(q_rot, kv_pages, lengths, req_dev, seq):
    q_local = q_rot.shape[1]
    heads = q_local // HD
    pages = seq // PAGE
    blk = pl.BlockSpec((seq, HD), lambda r, h, L: (r, h))
    page_blk = lambda which: pl.BlockSpec((pages, None, PAGE, HD), lambda r, h, L: (r, which, 0, h))
    steps = req_dev * heads
    cost = pl.CostEstimate(flops=steps * 4 * seq * seq * HD, transcendentals=steps * seq * seq,
                           bytes_accessed=steps * seq * HD * 2 * 4)
    return pl.pallas_call(
        attn_kernel,
        grid_spec=pltpu.PrefetchScalarGridSpec(
            num_scalar_prefetch=1, grid=(req_dev, heads), in_specs=[blk, page_blk(0), page_blk(1)], out_specs=blk),
        out_shape=jax.ShapeDtypeStruct((req_dev * seq, q_local), jnp.bfloat16),
        cost_estimate=cost,
        name="causal_attention",
    )(lengths, q_rot, kv_pages, kv_pages)


def extended(block, sides, width):
    for axis, dim in sides:
        count = lax.psum(1, axis)
        forward = [(i, i + 1) for i in range(count - 1)]
        forward.append((count - 1, 0))
        backward = [(target, source) for source, target in forward]
        low = lax.ppermute(
            lax.slice_in_dim(block, block.shape[dim] - width, None, axis=dim), axis, forward
        )
        high = lax.ppermute(lax.slice_in_dim(block, 0, width, axis=dim), axis, backward)
        block = jnp.concatenate([low, block, high], axis=dim)
    return block


def rotate(values_in, seq_len, head_size):
    half_size = head_size // 2
    positions = jnp.arange(seq_len).astype(jnp.float32)
    frequency = rope_theta ** (-jnp.arange(half_size).astype(jnp.float32) * 2.0 / head_size)
    angles = positions[:, None] * frequency[None, :]
    cosine_table = jnp.cos(angles)[:, None, :]
    sine_table = jnp.sin(angles)[:, None, :]
    front_half = values_in[..., :half_size]
    back_half = values_in[..., half_size:]
    return jnp.concatenate(
        [
            front_half * cosine_table - back_half * sine_table,
            back_half * cosine_table + front_half * sine_table,
        ],
        -1,
    )


def attend(request_item):
    queries, key_rows, value_rows, length = request_item
    seq_len = queries.shape[0]
    scores = jnp.einsum(
        "thd,uhd->htu", queries, key_rows, preferred_element_type=jnp.float32
    ) * HD ** (-0.5)
    query_pos = jnp.arange(seq_len)[:, None]
    key_pos = jnp.arange(seq_len)[None, :]
    allowed = (key_pos <= query_pos) & (key_pos < length)
    scores = jnp.where(allowed[None], scores, -1e30)
    row_max = jnp.max(scores, axis=-1, keepdims=True)
    exp_terms = jnp.where(allowed[None], jnp.exp(scores - row_max), 0.0)
    probs = (exp_terms / jnp.sum(exp_terms, axis=-1, keepdims=True)).astype(jnp.bfloat16)
    output = jnp.einsum("htu,uhd->thd", probs, value_rows, preferred_element_type=jnp.float32)
    keep_rows = jnp.arange(seq_len)[:, None, None] < length
    return jnp.where(keep_rows, output, 0.0).astype(jnp.bfloat16)


def body(tokens, qkv_master, q_gain, k_gain, lengths, page_holder, page_slot):
    req_dev, seq_len, model_width = tokens.shape
    row_share, _, q_local = qkv_master.shape
    heads_local = q_local // HD
    token_rows = tokens.reshape(req_dev * seq_len, model_width)
    master_local = qkv_master.astype(jnp.bfloat16).reshape(row_share, 3 * q_local)
    gathered = weight_gather(master_local).reshape(-1, master_local.shape[-1])
    projected = jnp.dot(token_rows, gathered, preferred_element_type=jnp.float32)
    square_sums = lax.psum(
        (
            jnp.sum(projected[:, :q_local] * projected[:, :q_local], -1),
            jnp.sum(projected[:, q_local : 2 * q_local] * projected[:, q_local : 2 * q_local], -1),
        ),
        "tp",
    )
    full_width = q_local * lax.axis_size("tp")
    q_scale = lax.rsqrt(square_sums[0] / full_width + norm_epsilon)[:, None]
    k_scale = lax.rsqrt(square_sums[1] / full_width + norm_epsilon)[:, None]
    half_size = HD // 2
    positions = jnp.arange(seq_len).astype(jnp.float32)
    frequency = rope_theta ** (-jnp.arange(half_size).astype(jnp.float32) * 2.0 / HD)
    angles = positions[:, None] * frequency[None, :]
    cosine, sine = jnp.cos(angles), jnp.sin(angles)
    cos_full = jnp.concatenate([cosine, cosine], -1)
    sin_signed = jnp.concatenate([-sine, sine], -1)
    q_flat, kv_pages = rope_and_round(
        projected, q_scale, k_scale, q_gain[None], k_gain[None], cos_full, sin_signed, req_dev, seq_len
    )
    attended = causal_attention(q_flat, kv_pages, lengths, req_dev, seq_len)
    attended = attended.reshape(req_dev, seq_len, q_local)
    page_count = seq_len // PAGE
    home_index = lax.axis_index(REQ)
    axis_count = lax.psum(1, REQ)
    is_live = (jnp.arange(page_count) * PAGE)[None, :] < lengths[:, None]
    offset = (page_holder - home_index + 1 + axis_count) % axis_count - 1
    target = jnp.where(is_live, (offset + 1) * CAP + page_slot, -1).reshape(-1)
    onehot = (target[None, :] == jnp.arange(SLOTS)[:, None]).astype(jnp.bfloat16)
    stacked = kv_pages.reshape(req_dev * page_count, 2 * PAGE * q_local)
    outgoing = (
        jnp.dot(onehot, stacked, preferred_element_type=jnp.float32)
        .astype(jnp.bfloat16)
        .reshape(SLOTS, 2, PAGE, q_local)
    )
    padded = extended(outgoing, ((REQ, 0),), CAP)
    kv_cache = jnp.concatenate([padded[CAP + SLOTS :], outgoing[CAP : 2 * CAP], padded[:CAP]], 0)
    return (attended, kv_cache)


REQ = ("yh", "z", "x", "c")


def solution(mesh):
    fine = Mesh(np.asarray(mesh.devices).reshape(2, 8, 4, 2, mesh.shape["tp"]), REQ + ("tp",))
    in_specs = (
        P(REQ, None, None),
        P(REQ, None, "tp"),
        P("tp"),
        P("tp"),
        P(REQ),
        P(REQ, None),
        P(REQ, None),
    )
    out_specs = (P(REQ, None, "tp"), P(REQ, None, None, "tp"))
    return jax.shard_map(body, mesh=fine, in_specs=in_specs, out_specs=out_specs, check_vma=False)
```

```python
import jax
import jax.numpy as jnp
from jax import lax
from jax.experimental import pallas as pl
from jax.experimental.pallas import tpu as pltpu
import numpy as np
from jax.sharding import Mesh, PartitionSpec as P

HD = 128
ROPE_WIDTH = 1024
PAGE = 128
CAP = 3
SLOTS = 9


norm_epsilon = 1e-06
rope_theta = 500000.0


def _put(out, piece, idx, at, col=0):
    starts = [0] * out.ndim
    starts[at] = idx
    starts[-1] = col
    return lax.dynamic_update_slice(out, jnp.expand_dims(piece, at), starts)

def ring_gather(x, axis, n, me, at=0):
    if n == 2:
        other = lax.ppermute(x, axis, [(0, 1), (1, 0)])
        return jnp.where(me == 0, jnp.stack([x, other], axis=at), jnp.stack([other, x], axis=at))
    out = jnp.zeros(x.shape[:at] + (n,) + x.shape[at:], x.dtype)
    out = _put(out, x, me, at)
    fwd = [(i, (i + 1) % n) for i in range(n)]
    bwd = [((i + 1) % n, i) for i in range(n)]
    left, right = x, x
    half = n // 2
    for s in range(1, (n + 1) // 2):
        left = lax.ppermute(left, axis, fwd)
        right = lax.ppermute(right, axis, bwd)
        out = _put(out, left, (me - s) % n, at)
        out = _put(out, right, (me + s) % n, at)
    if n % 2 == 0:
        h = x.shape[-1] // 2
        a = lax.ppermute(left[..., :h], axis, fwd)
        b = lax.ppermute(right[..., h:], axis, bwd)
        j = (me + half) % n
        out = _put(out, a, j, at, 0)
        out = _put(out, b, j, at, h)
    return out

def weight_gather(b):
    yh, z, x, c = (lax.axis_index(a) for a in ("yh", "z", "x", "c"))
    g = ring_gather(b, "yh", 2, yh)
    ga = ring_gather(g[0], "x", 4, x)
    ga = ring_gather(ga, "z", 8, z)
    gb = ring_gather(g[1], "z", 8, z)
    gb = ring_gather(gb, "x", 4, x, at=1)
    own = jnp.stack([ga, gb])
    return ring_gather(own, "c", 2, c, at=3)


def rope_kernel(q_ref, k_ref, v_ref, rq_ref, rk_ref, gq_ref, gk_ref, cos_ref, sin_ref, qrot_ref, kv_ref):
    cos = cos_ref[...]
    sin = sin_ref[...]
    width = cos.shape[1]
    lane = lax.broadcasted_iota(jnp.int32, cos.shape, 1)
    partner = jnp.where(lane % HD < HD // 2, lane + HD // 2, lane - HD // 2)
    from_first = pltpu.roll(lane, HD // 2, 1) == partner

    def rotated(x):
        swapped = jnp.where(from_first, pltpu.roll(x, HD // 2, 1), pltpu.roll(x, width - HD // 2, 1))
        return x * cos + swapped * sin

    q = q_ref[...] * rq_ref[...] * gq_ref[...]
    k = k_ref[...] * rk_ref[...] * gk_ref[...]
    qrot_ref[...] = rotated(q).astype(jnp.bfloat16)
    pages = kv_ref.shape[0]
    kv_ref[:, 0, :, :] = rotated(k).astype(jnp.bfloat16).reshape(pages, -1, width)
    kv_ref[:, 1, :, :] = v_ref[...].astype(jnp.bfloat16).reshape(pages, -1, width)


def attn_kernel(len_ref, q_ref, k_ref, v_ref, att_ref):
    length = len_ref[pl.program_id(0)]
    seq = q_ref.shape[0]
    keys = k_ref[...].reshape(seq, -1)
    vals = v_ref[...].reshape(seq, -1)
    scores = lax.dot_general(q_ref[...], keys, (((1,), (1,)), ((), ())),
                             preferred_element_type=jnp.float32) * HD ** (-0.5)
    t = lax.broadcasted_iota(jnp.int32, (seq, seq), 0)
    u = lax.broadcasted_iota(jnp.int32, (seq, seq), 1)
    allowed = (u <= t) & (u < length)
    scores = jnp.where(allowed, scores, -1e30)
    row_max = jnp.max(scores, axis=-1, keepdims=True)
    exp_terms = jnp.where(allowed, jnp.exp(scores - row_max), 0.0)
    probs = (exp_terms / jnp.sum(exp_terms, axis=-1, keepdims=True)).astype(jnp.bfloat16)
    out = jnp.dot(probs, vals, preferred_element_type=jnp.float32)
    rows = lax.broadcasted_iota(jnp.int32, (seq, 1), 0)
    att_ref[...] = jnp.where(rows < length, out, 0.0).astype(jnp.bfloat16)


def rope_and_round(projected, rq, rk, q_gain, k_gain, cos_full, sin_signed, req_dev, seq):
    q_local = projected.shape[1] // 3
    width = ROPE_WIDTH if q_local % ROPE_WIDTH == 0 else HD
    groups = q_local // width
    blk = lambda off: pl.BlockSpec((seq, width), lambda r, h: (r, off + h))
    row = pl.BlockSpec((seq, 1), lambda r, h: (r, 0))
    gain = pl.BlockSpec((1, width), lambda r, h: (0, h))
    table = pl.BlockSpec((seq, width), lambda r, h: (0, 0))
    out = pl.BlockSpec((seq, width), lambda r, h: (r, h))
    pages = seq // PAGE
    kv_out = pl.BlockSpec((pages, 2, PAGE, width), lambda r, h: (r, 0, 0, h))
    shape = jax.ShapeDtypeStruct((req_dev * seq, q_local), jnp.bfloat16)
    kv_shape = jax.ShapeDtypeStruct((req_dev * pages, 2, PAGE, q_local), jnp.bfloat16)
    reps = width // HD
    cos_full = jnp.tile(cos_full, (1, reps))
    sin_signed = jnp.tile(sin_signed, (1, reps))
    steps = req_dev * groups
    cost = pl.CostEstimate(flops=steps * seq * width * 12, transcendentals=0,
                           bytes_accessed=steps * seq * width * (3 * 4 + 3 * 2))
    return pl.pallas_call(
        rope_kernel,
        grid=(req_dev, groups),
        in_specs=[blk(0), blk(groups), blk(2 * groups), row, row, gain, gain, table, table],
        out_specs=[out, kv_out],
        out_shape=[shape, kv_shape],
        cost_estimate=cost,
        name="rope_and_round",
    )(projected, projected, projected, rq, rk, q_gain, k_gain, cos_full, sin_signed)


def causal_attention(q_rot, kv_pages, lengths, req_dev, seq):
    q_local = q_rot.shape[1]
    heads = q_local // HD
    pages = seq // PAGE
    blk = pl.BlockSpec((seq, HD), lambda r, h, L: (r, h))
    page_blk = lambda which: pl.BlockSpec((pages, None, PAGE, HD), lambda r, h, L: (r, which, 0, h))
    steps = req_dev * heads
    cost = pl.CostEstimate(flops=steps * 4 * seq * seq * HD, transcendentals=steps * seq * seq,
                           bytes_accessed=steps * seq * HD * 2 * 4)
    return pl.pallas_call(
        attn_kernel,
        grid_spec=pltpu.PrefetchScalarGridSpec(
            num_scalar_prefetch=1, grid=(req_dev, heads), in_specs=[blk, page_blk(0), page_blk(1)], out_specs=blk),
        out_shape=jax.ShapeDtypeStruct((req_dev * seq, q_local), jnp.bfloat16),
        cost_estimate=cost,
        name="causal_attention",
    )(lengths, q_rot, kv_pages, kv_pages)


def extended(block, sides, width):
    for axis, dim in sides:
        count = lax.psum(1, axis)
        forward = [(i, i + 1) for i in range(count - 1)]
        forward.append((count - 1, 0))
        backward = [(target, source) for source, target in forward]
        low = lax.ppermute(
            lax.slice_in_dim(block, block.shape[dim] - width, None, axis=dim), axis, forward
        )
        high = lax.ppermute(lax.slice_in_dim(block, 0, width, axis=dim), axis, backward)
        block = jnp.concatenate([low, block, high], axis=dim)
    return block


def rotate(values_in, seq_len, head_size):
    half_size = head_size // 2
    positions = jnp.arange(seq_len).astype(jnp.float32)
    frequency = rope_theta ** (-jnp.arange(half_size).astype(jnp.float32) * 2.0 / head_size)
    angles = positions[:, None] * frequency[None, :]
    cosine_table = jnp.cos(angles)[:, None, :]
    sine_table = jnp.sin(angles)[:, None, :]
    front_half = values_in[..., :half_size]
    back_half = values_in[..., half_size:]
    return jnp.concatenate(
        [
            front_half * cosine_table - back_half * sine_table,
            back_half * cosine_table + front_half * sine_table,
        ],
        -1,
    )


def attend(request_item):
    queries, key_rows, value_rows, length = request_item
    seq_len = queries.shape[0]
    scores = jnp.einsum(
        "thd,uhd->htu", queries, key_rows, preferred_element_type=jnp.float32
    ) * HD ** (-0.5)
    query_pos = jnp.arange(seq_len)[:, None]
    key_pos = jnp.arange(seq_len)[None, :]
    allowed = (key_pos <= query_pos) & (key_pos < length)
    scores = jnp.where(allowed[None], scores, -1e30)
    row_max = jnp.max(scores, axis=-1, keepdims=True)
    exp_terms = jnp.where(allowed[None], jnp.exp(scores - row_max), 0.0)
    probs = (exp_terms / jnp.sum(exp_terms, axis=-1, keepdims=True)).astype(jnp.bfloat16)
    output = jnp.einsum("htu,uhd->thd", probs, value_rows, preferred_element_type=jnp.float32)
    keep_rows = jnp.arange(seq_len)[:, None, None] < length
    return jnp.where(keep_rows, output, 0.0).astype(jnp.bfloat16)


def body(tokens, qkv_master, q_gain, k_gain, lengths, page_holder, page_slot):
    req_dev, seq_len, model_width = tokens.shape
    row_share, _, q_local = qkv_master.shape
    heads_local = q_local // HD
    token_rows = tokens.reshape(req_dev * seq_len, model_width)
    master_local = qkv_master.astype(jnp.bfloat16).reshape(row_share, 3 * q_local)
    gathered = weight_gather(master_local).reshape(-1, master_local.shape[-1])
    projected = jnp.dot(token_rows, gathered, preferred_element_type=jnp.float32)
    square_sums = lax.psum(
        (
            jnp.sum(projected[:, :q_local] * projected[:, :q_local], -1),
            jnp.sum(projected[:, q_local : 2 * q_local] * projected[:, q_local : 2 * q_local], -1),
        ),
        "tp",
    )
    full_width = q_local * lax.axis_size("tp")
    q_scale = lax.rsqrt(square_sums[0] / full_width + norm_epsilon)[:, None]
    k_scale = lax.rsqrt(square_sums[1] / full_width + norm_epsilon)[:, None]
    half_size = HD // 2
    positions = jnp.arange(seq_len).astype(jnp.float32)
    frequency = rope_theta ** (-jnp.arange(half_size).astype(jnp.float32) * 2.0 / HD)
    angles = positions[:, None] * frequency[None, :]
    cosine, sine = jnp.cos(angles), jnp.sin(angles)
    cos_full = jnp.concatenate([cosine, cosine], -1)
    sin_signed = jnp.concatenate([-sine, sine], -1)
    q_flat, kv_pages = rope_and_round(
        projected, q_scale, k_scale, q_gain[None], k_gain[None], cos_full, sin_signed, req_dev, seq_len
    )
    attended = causal_attention(q_flat, kv_pages, lengths, req_dev, seq_len)
    attended = attended.reshape(req_dev, seq_len, q_local)
    page_count = seq_len // PAGE
    home_index = lax.axis_index(REQ)
    axis_count = lax.psum(1, REQ)
    is_live = (jnp.arange(page_count) * PAGE)[None, :] < lengths[:, None]
    offset = (page_holder - home_index + 1 + axis_count) % axis_count - 1
    target = jnp.where(is_live, (offset + 1) * CAP + page_slot, -1).reshape(-1)
    onehot = (target[None, :] == jnp.arange(SLOTS)[:, None]).astype(jnp.bfloat16)
    stacked = kv_pages.reshape(req_dev * page_count, 2 * PAGE * q_local)
    outgoing = (
        jnp.dot(onehot, stacked, preferred_element_type=jnp.float32)
        .astype(jnp.bfloat16)
        .reshape(SLOTS, 2, PAGE, q_local)
    )
    padded = extended(outgoing, ((REQ, 0),), CAP)
    kv_cache = jnp.concatenate([padded[CAP + SLOTS :], outgoing[CAP : 2 * CAP], padded[:CAP]], 0)
    return (attended, kv_cache)


REQ = ("yh", "z", "x", "c")


def solution(mesh):
    fine = Mesh(np.asarray(mesh.devices).reshape(2, 8, 4, 2, mesh.shape["tp"]), REQ + ("tp",))
    in_specs = (
        P(REQ, None, None),
        P(REQ, None, "tp"),
        P("tp"),
        P("tp"),
        P(REQ),
        P(REQ, None),
        P(REQ, None),
    )
    out_specs = (P(REQ, None, "tp"), P(REQ, None, None, "tp"))
    return jax.shard_map(body, mesh=fine, in_specs=in_specs, out_specs=out_specs, check_vma=False)
```

```python
import jax
import jax.numpy as jnp
from jax import lax
from jax.experimental import pallas as pl
from jax.experimental.pallas import tpu as pltpu
import numpy as np
from jax.sharding import Mesh, PartitionSpec as P

HD = 128
ROPE_WIDTH = 512
PAGE = 128
CAP = 3
SLOTS = 9


norm_epsilon = 1e-06
rope_theta = 500000.0


def _put(out, piece, idx, at, col=0):
    starts = [0] * out.ndim
    starts[at] = idx
    starts[-1] = col
    return lax.dynamic_update_slice(out, jnp.expand_dims(piece, at), starts)

def ring_gather(x, axis, n, me, at=0):
    if n == 2:
        other = lax.ppermute(x, axis, [(0, 1), (1, 0)])
        return jnp.where(me == 0, jnp.stack([x, other], axis=at), jnp.stack([other, x], axis=at))
    out = jnp.zeros(x.shape[:at] + (n,) + x.shape[at:], x.dtype)
    out = _put(out, x, me, at)
    fwd = [(i, (i + 1) % n) for i in range(n)]
    bwd = [((i + 1) % n, i) for i in range(n)]
    left, right = x, x
    half = n // 2
    for s in range(1, (n + 1) // 2):
        left = lax.ppermute(left, axis, fwd)
        right = lax.ppermute(right, axis, bwd)
        out = _put(out, left, (me - s) % n, at)
        out = _put(out, right, (me + s) % n, at)
    if n % 2 == 0:
        h = x.shape[-1] // 2
        a = lax.ppermute(left[..., :h], axis, fwd)
        b = lax.ppermute(right[..., h:], axis, bwd)
        j = (me + half) % n
        out = _put(out, a, j, at, 0)
        out = _put(out, b, j, at, h)
    return out

def weight_gather(b):
    yh, z, x, c = (lax.axis_index(a) for a in ("yh", "z", "x", "c"))
    g = ring_gather(b, "yh", 2, yh)
    ga = ring_gather(g[0], "x", 4, x)
    ga = ring_gather(ga, "z", 8, z)
    gb = ring_gather(g[1], "z", 8, z)
    gb = ring_gather(gb, "x", 4, x, at=1)
    own = jnp.stack([ga, gb])
    return ring_gather(own, "c", 2, c, at=3)


def _rotated(x, cos, sin):
    width = cos.shape[1]
    lane = lax.broadcasted_iota(jnp.int32, cos.shape, 1)
    partner = jnp.where(lane % HD < HD // 2, lane + HD // 2, lane - HD // 2)
    from_first = pltpu.roll(lane, HD // 2, 1) == partner
    swapped = jnp.where(from_first, pltpu.roll(x, HD // 2, 1), pltpu.roll(x, width - HD // 2, 1))
    return x * cos + swapped * sin


def kv_rope_kernel(k_ref, v_ref, rk_ref, gk_ref, cos_ref, sin_ref, kv_ref):
    k = k_ref[...] * rk_ref[...] * gk_ref[...]
    pages = kv_ref.shape[0]
    width = cos_ref.shape[1]
    kv_ref[:, 0, :, :] = _rotated(k, cos_ref[...], sin_ref[...]).astype(jnp.bfloat16).reshape(pages, -1, width)
    kv_ref[:, 1, :, :] = v_ref[...].astype(jnp.bfloat16).reshape(pages, -1, width)


def q_rope_kernel(q_ref, rq_ref, gq_ref, cos_ref, sin_ref, qrot_ref):
    q = q_ref[...] * rq_ref[...] * gq_ref[...]
    qrot_ref[...] = _rotated(q, cos_ref[...], sin_ref[...]).astype(jnp.bfloat16)


def attn_kernel(len_ref, q_ref, k_ref, v_ref, att_ref):
    length = len_ref[pl.program_id(0)]
    seq = q_ref.shape[0]
    keys = k_ref[...].reshape(seq, -1)
    vals = v_ref[...].reshape(seq, -1)
    scores = lax.dot_general(q_ref[...], keys, (((1,), (1,)), ((), ())),
                             preferred_element_type=jnp.float32) * HD ** (-0.5)
    t = lax.broadcasted_iota(jnp.int32, (seq, seq), 0)
    u = lax.broadcasted_iota(jnp.int32, (seq, seq), 1)
    allowed = (u <= t) & (u < length)
    scores = jnp.where(allowed, scores, -1e30)
    row_max = jnp.max(scores, axis=-1, keepdims=True)
    exp_terms = jnp.where(allowed, jnp.exp(scores - row_max), 0.0)
    probs = (exp_terms / jnp.sum(exp_terms, axis=-1, keepdims=True)).astype(jnp.bfloat16)
    out = jnp.dot(probs, vals, preferred_element_type=jnp.float32)
    rows = lax.broadcasted_iota(jnp.int32, (seq, 1), 0)
    att_ref[...] = jnp.where(rows < length, out, 0.0).astype(jnp.bfloat16)


def rope_and_round(projected, rq, rk, q_gain, k_gain, cos_full, sin_signed, req_dev, seq):
    q_local = projected.shape[1] // 3
    width = ROPE_WIDTH if q_local % ROPE_WIDTH == 0 else HD
    groups = q_local // width
    blk = lambda off: pl.BlockSpec((seq, width), lambda r, h: (r, off + h))
    row = pl.BlockSpec((seq, 1), lambda r, h: (r, 0))
    gain = pl.BlockSpec((1, width), lambda r, h: (0, h))
    table = pl.BlockSpec((seq, width), lambda r, h: (0, 0))
    out = pl.BlockSpec((seq, width), lambda r, h: (r, h))
    pages = seq // PAGE
    kv_out = pl.BlockSpec((pages, 2, PAGE, width), lambda r, h: (r, 0, 0, h))
    shape = jax.ShapeDtypeStruct((req_dev * seq, q_local), jnp.bfloat16)
    kv_shape = jax.ShapeDtypeStruct((req_dev * pages, 2, PAGE, q_local), jnp.bfloat16)
    reps = width // HD
    cos_full = jnp.tile(cos_full, (1, reps))
    sin_signed = jnp.tile(sin_signed, (1, reps))
    steps = req_dev * groups
    kv_pages = pl.pallas_call(
        kv_rope_kernel,
        grid=(req_dev, groups),
        in_specs=[blk(groups), blk(2 * groups), row, gain, table, table],
        out_specs=kv_out,
        out_shape=kv_shape,
        cost_estimate=pl.CostEstimate(flops=steps * seq * width * 8, transcendentals=0,
                                      bytes_accessed=steps * seq * width * (2 * 4 + 2 * 2)),
        name="kv_rope",
    )(projected, projected, rk, k_gain, cos_full, sin_signed)
    q_rot = pl.pallas_call(
        q_rope_kernel,
        grid=(req_dev, groups),
        in_specs=[blk(0), row, gain, table, table],
        out_specs=out,
        out_shape=shape,
        cost_estimate=pl.CostEstimate(flops=steps * seq * width * 8, transcendentals=0,
                                      bytes_accessed=steps * seq * width * (4 + 2)),
        name="q_rope",
    )(projected, rq, q_gain, cos_full, sin_signed)
    return q_rot, kv_pages


def causal_attention(q_rot, kv_pages, lengths, req_dev, seq):
    q_local = q_rot.shape[1]
    heads = q_local // HD
    pages = seq // PAGE
    blk = pl.BlockSpec((seq, HD), lambda r, h, L: (r, h))
    page_blk = lambda which: pl.BlockSpec((pages, None, PAGE, HD), lambda r, h, L: (r, which, 0, h))
    steps = req_dev * heads
    cost = pl.CostEstimate(flops=steps * 4 * seq * seq * HD, transcendentals=steps * seq * seq,
                           bytes_accessed=steps * seq * HD * 2 * 4)
    return pl.pallas_call(
        attn_kernel,
        grid_spec=pltpu.PrefetchScalarGridSpec(
            num_scalar_prefetch=1, grid=(req_dev, heads), in_specs=[blk, page_blk(0), page_blk(1)], out_specs=blk),
        out_shape=jax.ShapeDtypeStruct((req_dev * seq, q_local), jnp.bfloat16),
        cost_estimate=cost,
        name="causal_attention",
    )(lengths, q_rot, kv_pages, kv_pages)


def extended(block, sides, width):
    for axis, dim in sides:
        count = lax.psum(1, axis)
        forward = [(i, i + 1) for i in range(count - 1)]
        forward.append((count - 1, 0))
        backward = [(target, source) for source, target in forward]
        low = lax.ppermute(
            lax.slice_in_dim(block, block.shape[dim] - width, None, axis=dim), axis, forward
        )
        high = lax.ppermute(lax.slice_in_dim(block, 0, width, axis=dim), axis, backward)
        block = jnp.concatenate([low, block, high], axis=dim)
    return block


def rotate(values_in, seq_len, head_size):
    half_size = head_size // 2
    positions = jnp.arange(seq_len).astype(jnp.float32)
    frequency = rope_theta ** (-jnp.arange(half_size).astype(jnp.float32) * 2.0 / head_size)
    angles = positions[:, None] * frequency[None, :]
    cosine_table = jnp.cos(angles)[:, None, :]
    sine_table = jnp.sin(angles)[:, None, :]
    front_half = values_in[..., :half_size]
    back_half = values_in[..., half_size:]
    return jnp.concatenate(
        [
            front_half * cosine_table - back_half * sine_table,
            back_half * cosine_table + front_half * sine_table,
        ],
        -1,
    )


def attend(request_item):
    queries, key_rows, value_rows, length = request_item
    seq_len = queries.shape[0]
    scores = jnp.einsum(
        "thd,uhd->htu", queries, key_rows, preferred_element_type=jnp.float32
    ) * HD ** (-0.5)
    query_pos = jnp.arange(seq_len)[:, None]
    key_pos = jnp.arange(seq_len)[None, :]
    allowed = (key_pos <= query_pos) & (key_pos < length)
    scores = jnp.where(allowed[None], scores, -1e30)
    row_max = jnp.max(scores, axis=-1, keepdims=True)
    exp_terms = jnp.where(allowed[None], jnp.exp(scores - row_max), 0.0)
    probs = (exp_terms / jnp.sum(exp_terms, axis=-1, keepdims=True)).astype(jnp.bfloat16)
    output = jnp.einsum("htu,uhd->thd", probs, value_rows, preferred_element_type=jnp.float32)
    keep_rows = jnp.arange(seq_len)[:, None, None] < length
    return jnp.where(keep_rows, output, 0.0).astype(jnp.bfloat16)


def body(tokens, qkv_master, q_gain, k_gain, lengths, page_holder, page_slot):
    req_dev, seq_len, model_width = tokens.shape
    row_share, _, q_local = qkv_master.shape
    heads_local = q_local // HD
    token_rows = tokens.reshape(req_dev * seq_len, model_width)
    master_local = qkv_master.astype(jnp.bfloat16).reshape(row_share, 3 * q_local)
    gathered = weight_gather(master_local).reshape(-1, master_local.shape[-1])
    projected = jnp.dot(token_rows, gathered, preferred_element_type=jnp.float32)
    square_sums = lax.psum(
        (
            jnp.sum(projected[:, :q_local] * projected[:, :q_local], -1),
            jnp.sum(projected[:, q_local : 2 * q_local] * projected[:, q_local : 2 * q_local], -1),
        ),
        "tp",
    )
    full_width = q_local * lax.axis_size("tp")
    q_scale = lax.rsqrt(square_sums[0] / full_width + norm_epsilon)[:, None]
    k_scale = lax.rsqrt(square_sums[1] / full_width + norm_epsilon)[:, None]
    half_size = HD // 2
    positions = jnp.arange(seq_len).astype(jnp.float32)
    frequency = rope_theta ** (-jnp.arange(half_size).astype(jnp.float32) * 2.0 / HD)
    angles = positions[:, None] * frequency[None, :]
    cosine, sine = jnp.cos(angles), jnp.sin(angles)
    cos_full = jnp.concatenate([cosine, cosine], -1)
    sin_signed = jnp.concatenate([-sine, sine], -1)
    q_flat, kv_pages = rope_and_round(
        projected, q_scale, k_scale, q_gain[None], k_gain[None], cos_full, sin_signed, req_dev, seq_len
    )
    attended = causal_attention(q_flat, kv_pages, lengths, req_dev, seq_len)
    attended = attended.reshape(req_dev, seq_len, q_local)
    page_count = seq_len // PAGE
    home_index = lax.axis_index(REQ)
    axis_count = lax.psum(1, REQ)
    is_live = (jnp.arange(page_count) * PAGE)[None, :] < lengths[:, None]
    offset = (page_holder - home_index + 1 + axis_count) % axis_count - 1
    target = jnp.where(is_live, (offset + 1) * CAP + page_slot, -1).reshape(-1)
    onehot = (target[None, :] == jnp.arange(SLOTS)[:, None]).astype(jnp.bfloat16)
    stacked = kv_pages.reshape(req_dev * page_count, 2 * PAGE * q_local)
    outgoing = (
        jnp.dot(onehot, stacked, preferred_element_type=jnp.float32)
        .astype(jnp.bfloat16)
        .reshape(SLOTS, 2, PAGE, q_local)
    )
    padded = extended(outgoing, ((REQ, 0),), CAP)
    kv_cache = jnp.concatenate([padded[CAP + SLOTS :], outgoing[CAP : 2 * CAP], padded[:CAP]], 0)
    return (attended, kv_cache)


REQ = ("yh", "z", "x", "c")


def solution(mesh):
    fine = Mesh(np.asarray(mesh.devices).reshape(2, 8, 4, 2, mesh.shape["tp"]), REQ + ("tp",))
    in_specs = (
        P(REQ, None, None),
        P(REQ, None, "tp"),
        P("tp"),
        P("tp"),
        P(REQ),
        P(REQ, None),
        P(REQ, None),
    )
    out_specs = (P(REQ, None, "tp"), P(REQ, None, None, "tp"))
    return jax.shard_map(body, mesh=fine, in_specs=in_specs, out_specs=out_specs, check_vma=False)
```

```python
import jax
import jax.numpy as jnp
from jax import lax
from jax.experimental import pallas as pl
from jax.experimental.pallas import tpu as pltpu
import numpy as np
from jax.sharding import Mesh, PartitionSpec as P

HD = 128
ROPE_WIDTH = 512
PAGE = 128
CAP = 3
SLOTS = 9


norm_epsilon = 1e-06
rope_theta = 500000.0


def _put(out, piece, idx, at, col=0):
    starts = [0] * out.ndim
    starts[at] = idx
    starts[-1] = col
    return lax.dynamic_update_slice(out, jnp.expand_dims(piece, at), starts)

def ring_gather(x, axis, n, me, at=0):
    if n == 2:
        other = lax.ppermute(x, axis, [(0, 1), (1, 0)])
        return jnp.where(me == 0, jnp.stack([x, other], axis=at), jnp.stack([other, x], axis=at))
    out = jnp.zeros(x.shape[:at] + (n,) + x.shape[at:], x.dtype)
    out = _put(out, x, me, at)
    fwd = [(i, (i + 1) % n) for i in range(n)]
    bwd = [((i + 1) % n, i) for i in range(n)]
    left, right = x, x
    half = n // 2
    for s in range(1, (n + 1) // 2):
        left = lax.ppermute(left, axis, fwd)
        right = lax.ppermute(right, axis, bwd)
        out = _put(out, left, (me - s) % n, at)
        out = _put(out, right, (me + s) % n, at)
    if n % 2 == 0:
        h = x.shape[-1] // 2
        a = lax.ppermute(left[..., :h], axis, fwd)
        b = lax.ppermute(right[..., h:], axis, bwd)
        j = (me + half) % n
        out = _put(out, a, j, at, 0)
        out = _put(out, b, j, at, h)
    return out

def weight_gather(b):
    yh, z, x, c = (lax.axis_index(a) for a in ("yh", "z", "x", "c"))
    g = ring_gather(b, "yh", 2, yh)
    ga = ring_gather(g[0], "x", 4, x)
    ga = ring_gather(ga, "z", 8, z)
    gb = ring_gather(g[1], "z", 8, z)
    gb = ring_gather(gb, "x", 4, x, at=1)
    own = jnp.stack([ga, gb])
    return ring_gather(own, "c", 2, c, at=3)


def rope_kernel(q_ref, k_ref, v_ref, rq_ref, rk_ref, gq_ref, gk_ref, cos_ref, sin_ref, qrot_ref, kv_ref):
    cos = cos_ref[...]
    sin = sin_ref[...]
    width = cos.shape[1]
    lane = lax.broadcasted_iota(jnp.int32, cos.shape, 1)
    partner = jnp.where(lane % HD < HD // 2, lane + HD // 2, lane - HD // 2)
    from_first = pltpu.roll(lane, HD // 2, 1) == partner

    def rotated(x):
        swapped = jnp.where(from_first, pltpu.roll(x, HD // 2, 1), pltpu.roll(x, width - HD // 2, 1))
        return x * cos + swapped * sin

    q = q_ref[...] * rq_ref[...] * gq_ref[...]
    k = k_ref[...] * rk_ref[...] * gk_ref[...]
    qrot_ref[...] = rotated(q).astype(jnp.bfloat16)
    pages = kv_ref.shape[0]
    kv_ref[:, 0, :, :] = rotated(k).astype(jnp.bfloat16).reshape(pages, -1, width)
    kv_ref[:, 1, :, :] = v_ref[...].astype(jnp.bfloat16).reshape(pages, -1, width)


def attn_kernel(len_ref, q_ref, k_ref, v_ref, att_ref):
    length = len_ref[pl.program_id(0)]
    seq = q_ref.shape[0]
    keys = k_ref[...].reshape(seq, -1)
    vals = v_ref[...].reshape(seq, -1)
    scores = lax.dot_general(q_ref[...], keys, (((1,), (1,)), ((), ())),
                             preferred_element_type=jnp.float32) * HD ** (-0.5)
    t = lax.broadcasted_iota(jnp.int32, (seq, seq), 0)
    u = lax.broadcasted_iota(jnp.int32, (seq, seq), 1)
    allowed = (u <= t) & (u < length)
    scores = jnp.where(allowed, scores, -1e30)
    row_max = jnp.max(scores, axis=-1, keepdims=True)
    exp_terms = jnp.where(allowed, jnp.exp(scores - row_max), 0.0)
    probs = (exp_terms / jnp.sum(exp_terms, axis=-1, keepdims=True)).astype(jnp.bfloat16)
    out = jnp.dot(probs, vals, preferred_element_type=jnp.float32)
    rows = lax.broadcasted_iota(jnp.int32, (seq, 1), 0)
    att_ref[...] = jnp.where(rows < length, out, 0.0).astype(jnp.bfloat16)


def rope_and_round(projected, rq, rk, q_gain, k_gain, cos_full, sin_signed, req_dev, seq):
    q_local = projected.shape[1] // 3
    width = ROPE_WIDTH if q_local % ROPE_WIDTH == 0 else HD
    groups = q_local // width
    blk = lambda off: pl.BlockSpec((seq, width), lambda r, h: (r, off + h))
    row = pl.BlockSpec((seq, 1), lambda r, h: (r, 0))
    gain = pl.BlockSpec((1, width), lambda r, h: (0, h))
    table = pl.BlockSpec((seq, width), lambda r, h: (0, 0))
    out = pl.BlockSpec((seq, width), lambda r, h: (r, h))
    pages = seq // PAGE
    kv_out = pl.BlockSpec((pages, 2, PAGE, width), lambda r, h: (r, 0, 0, h))
    shape = jax.ShapeDtypeStruct((req_dev * seq, q_local), jnp.bfloat16)
    kv_shape = jax.ShapeDtypeStruct((req_dev * pages, 2, PAGE, q_local), jnp.bfloat16)
    reps = width // HD
    cos_full = jnp.tile(cos_full, (1, reps))
    sin_signed = jnp.tile(sin_signed, (1, reps))
    steps = req_dev * groups
    cost = pl.CostEstimate(flops=steps * seq * width * 12, transcendentals=0,
                           bytes_accessed=steps * seq * width * (3 * 4 + 3 * 2))
    return pl.pallas_call(
        rope_kernel,
        grid=(req_dev, groups),
        in_specs=[blk(0), blk(groups), blk(2 * groups), row, row, gain, gain, table, table],
        out_specs=[out, kv_out],
        out_shape=[shape, kv_shape],
        cost_estimate=cost,
        name="rope_and_round",
    )(projected, projected, projected, rq, rk, q_gain, k_gain, cos_full, sin_signed)


def causal_attention(q_rot, kv_pages, lengths, req_dev, seq):
    q_local = q_rot.shape[1]
    heads = q_local // HD
    pages = seq // PAGE
    blk = pl.BlockSpec((seq, HD), lambda r, h, L: (r, h))
    page_blk = lambda which: pl.BlockSpec((pages, None, PAGE, HD), lambda r, h, L: (r, which, 0, h))
    steps = req_dev * heads
    cost = pl.CostEstimate(flops=steps * 4 * seq * seq * HD, transcendentals=steps * seq * seq,
                           bytes_accessed=steps * seq * HD * 2 * 4)
    return pl.pallas_call(
        attn_kernel,
        grid_spec=pltpu.PrefetchScalarGridSpec(
            num_scalar_prefetch=1, grid=(req_dev, heads), in_specs=[blk, page_blk(0), page_blk(1)], out_specs=blk),
        out_shape=jax.ShapeDtypeStruct((req_dev * seq, q_local), jnp.bfloat16),
        cost_estimate=cost,
        name="causal_attention",
    )(lengths, q_rot, kv_pages, kv_pages)


def extended(block, sides, width):
    for axis, dim in sides:
        count = lax.psum(1, axis)
        forward = [(i, i + 1) for i in range(count - 1)]
        forward.append((count - 1, 0))
        backward = [(target, source) for source, target in forward]
        low = lax.ppermute(
            lax.slice_in_dim(block, block.shape[dim] - width, None, axis=dim), axis, forward
        )
        high = lax.ppermute(lax.slice_in_dim(block, 0, width, axis=dim), axis, backward)
        block = jnp.concatenate([low, block, high], axis=dim)
    return block


def rotate(values_in, seq_len, head_size):
    half_size = head_size // 2
    positions = jnp.arange(seq_len).astype(jnp.float32)
    frequency = rope_theta ** (-jnp.arange(half_size).astype(jnp.float32) * 2.0 / head_size)
    angles = positions[:, None] * frequency[None, :]
    cosine_table = jnp.cos(angles)[:, None, :]
    sine_table = jnp.sin(angles)[:, None, :]
    front_half = values_in[..., :half_size]
    back_half = values_in[..., half_size:]
    return jnp.concatenate(
        [
            front_half * cosine_table - back_half * sine_table,
            back_half * cosine_table + front_half * sine_table,
        ],
        -1,
    )


def attend(request_item):
    queries, key_rows, value_rows, length = request_item
    seq_len = queries.shape[0]
    scores = jnp.einsum(
        "thd,uhd->htu", queries, key_rows, preferred_element_type=jnp.float32
    ) * HD ** (-0.5)
    query_pos = jnp.arange(seq_len)[:, None]
    key_pos = jnp.arange(seq_len)[None, :]
    allowed = (key_pos <= query_pos) & (key_pos < length)
    scores = jnp.where(allowed[None], scores, -1e30)
    row_max = jnp.max(scores, axis=-1, keepdims=True)
    exp_terms = jnp.where(allowed[None], jnp.exp(scores - row_max), 0.0)
    probs = (exp_terms / jnp.sum(exp_terms, axis=-1, keepdims=True)).astype(jnp.bfloat16)
    output = jnp.einsum("htu,uhd->thd", probs, value_rows, preferred_element_type=jnp.float32)
    keep_rows = jnp.arange(seq_len)[:, None, None] < length
    return jnp.where(keep_rows, output, 0.0).astype(jnp.bfloat16)


def body(tokens, qkv_master, q_gain, k_gain, lengths, page_holder, page_slot):
    req_dev, seq_len, model_width = tokens.shape
    row_share, _, q_local = qkv_master.shape
    heads_local = q_local // HD
    token_rows = tokens.reshape(req_dev * seq_len, model_width)
    master_local = qkv_master.astype(jnp.bfloat16).reshape(row_share, 3 * q_local)
    gathered = weight_gather(master_local).reshape(-1, master_local.shape[-1])
    projected = jnp.dot(token_rows, gathered, preferred_element_type=jnp.float32)
    local_sums = jnp.stack(
        [
            jnp.sum(projected[:, :q_local] * projected[:, :q_local], -1),
            jnp.sum(projected[:, q_local : 2 * q_local] * projected[:, q_local : 2 * q_local], -1),
        ]
    )
    square_sums = local_sums + lax.ppermute(local_sums, "tp", [(0, 1), (1, 0)])
    full_width = q_local * lax.axis_size("tp")
    q_scale = lax.rsqrt(square_sums[0] / full_width + norm_epsilon)[:, None]
    k_scale = lax.rsqrt(square_sums[1] / full_width + norm_epsilon)[:, None]
    half_size = HD // 2
    positions = jnp.arange(seq_len).astype(jnp.float32)
    frequency = rope_theta ** (-jnp.arange(half_size).astype(jnp.float32) * 2.0 / HD)
    angles = positions[:, None] * frequency[None, :]
    cosine, sine = jnp.cos(angles), jnp.sin(angles)
    cos_full = jnp.concatenate([cosine, cosine], -1)
    sin_signed = jnp.concatenate([-sine, sine], -1)
    q_flat, kv_pages = rope_and_round(
        projected, q_scale, k_scale, q_gain[None], k_gain[None], cos_full, sin_signed, req_dev, seq_len
    )
    attended = causal_attention(q_flat, kv_pages, lengths, req_dev, seq_len)
    attended = attended.reshape(req_dev, seq_len, q_local)
    page_count = seq_len // PAGE
    home_index = lax.axis_index(REQ)
    axis_count = lax.psum(1, REQ)
    is_live = (jnp.arange(page_count) * PAGE)[None, :] < lengths[:, None]
    offset = (page_holder - home_index + 1 + axis_count) % axis_count - 1
    target = jnp.where(is_live, (offset + 1) * CAP + page_slot, -1).reshape(-1)
    onehot = (target[None, :] == jnp.arange(SLOTS)[:, None]).astype(jnp.bfloat16)
    stacked = kv_pages.reshape(req_dev * page_count, 2 * PAGE * q_local)
    outgoing = (
        jnp.dot(onehot, stacked, preferred_element_type=jnp.float32)
        .astype(jnp.bfloat16)
        .reshape(SLOTS, 2, PAGE, q_local)
    )
    padded = extended(outgoing, ((REQ, 0),), CAP)
    kv_cache = jnp.concatenate([padded[CAP + SLOTS :], outgoing[CAP : 2 * CAP], padded[:CAP]], 0)
    return (attended, kv_cache)


REQ = ("yh", "z", "x", "c")


def solution(mesh):
    fine = Mesh(np.asarray(mesh.devices).reshape(2, 8, 4, 2, mesh.shape["tp"]), REQ + ("tp",))
    in_specs = (
        P(REQ, None, None),
        P(REQ, None, "tp"),
        P("tp"),
        P("tp"),
        P(REQ),
        P(REQ, None),
        P(REQ, None),
    )
    out_specs = (P(REQ, None, "tp"), P(REQ, None, None, "tp"))
    return jax.shard_map(body, mesh=fine, in_specs=in_specs, out_specs=out_specs, check_vma=False)
```
